256 devices in a mesh: rep: 2 (over y_hi), fsdp: 64 (over x, z, y_lo), tp: 2 (over core).
Axes of the slice: x: 4, y: 4 (y_hi: 2, y_lo: 2; y = y_hi * 2 + y_lo), z: 8, core: 2. Of those that a mesh axis runs over, the one named last changes fastest.
Arguments:
- attn_global: float32 [24, 1024, 1024], P('rep', 'fsdp', 'tp'), may hold values from -6 to 6
- attn_momentum: float32 [24, 1024, 1024], P('rep', 'fsdp', 'tp'), may hold values from -6 to 6
- attn_inner: bfloat16 [2, 24, 1024, 1024], P('rep', None, 'fsdp', 'tp'), may hold values from -6 to 6
- norm_global: float32 [4, 1024], P('rep', 'tp'), may hold values from 0.5 to 1.5
- norm_momentum: float32 [4, 1024], P('rep', 'tp'), may hold values from -4 to 4
- norm_inner: bfloat16 [2, 4, 1024], P('rep', None, 'tp'), may hold values from 0.5 to 1.5
- emb_global: float32 [64, 2, 251, 1024], P('fsdp', 'rep', None, 'tp'), may hold values from -6 to 6
- emb_momentum: float32 [64, 2, 251, 1024], P('fsdp', 'rep', None, 'tp'), may hold values from -6 to 6
- emb_inner: bfloat16 [2, 32128, 1024], P('rep', 'fsdp', 'tp'), may hold values from -6 to 6
- basis: float32 [1024, 64], replicated, may hold values from -0.1875 to 0.1875
- touched: int32 [2, 8192], replicated, may hold values from 0 to 32127
Outputs:
- new_attn_global: float32 [24, 1024, 1024], P('rep', 'fsdp', 'tp')
- new_attn_momentum: float32 [24, 1024, 1024], P('rep', 'fsdp', 'tp')
- attn_weights: float32 [24, 1024, 1024], P(None, 'fsdp', 'tp')
- new_norm_global: float32 [4, 1024], P('rep', 'tp')
- new_norm_momentum: float32 [4, 1024], P('rep', 'tp')
- norm_weights: float32 [4, 1024], P(None, 'tp')
- new_emb_global: float32 [64, 2, 251, 1024], P('fsdp', 'rep', None, 'tp')
- new_emb_momentum: float32 [64, 2, 251, 1024], P('fsdp', 'rep', None, 'tp')
- emb_weights: float32 [32128, 1024], P('fsdp', 'tp')
The draws below stay inside these ranges and needn't reach their ends.
All inputs are finite; a program needn't handle non-finite values.
Results may differ from the reference program's by a relative error of at most 0.0003.
Values sent between devices are 32-bit elements; how exact they have to be, the bound alone decides.
No kernel may reach another device: no remote copies, remote signals or barrier semaphores. Data moves between devices by JAX's collectives and lax.ppermute only.
A program may use at most 64 MiB of HBM per device.

```python
import jax
import jax.numpy as jnp
from jax import lax

D = 1024
VOCAB = 32128
RANK = 64
MATS = 24
NORMS = 4
TOUCHED = 8192
REPS = 2
EMB_BLOCKS = 64
EMB_ROWS = 251


def touch_ends(drawn, own_key, smallest, high):
    shape = drawn.shape
    index_at = [jax.random.randint(jax.random.fold_in(own_key, axis), (), 0, shape[axis]) for axis in range(len(shape))]
    drawn = drawn.at[tuple(index_at)].set(smallest)
    longest = shape.index(max(shape))
    index_at[longest] = (index_at[longest] + 1) % shape[longest]
    return drawn.at[tuple(index_at)].set(high)


def shard_levels(own_key, dims, split, low, top_value):
    def one(axis_at, parts):
        draws = jax.random.uniform(jax.random.fold_in(jax.random.fold_in(own_key, 6), axis_at), (parts,), jnp.float32, low / len(split), top_value / len(split))
        return jnp.repeat(jnp.exp(draws), dims[axis_at] // parts).reshape((-1,) + (1,) * (len(dims) - axis_at - 1))

    loudness = one(*split[0])
    for cut in split[1:]:
        loudness = loudness * one(*cut)
    return loudness


def bell_draw(rng, extent, scale, reach, split=(), kind=jnp.bfloat16):
    result = jax.random.normal(rng, extent, jnp.float32) * scale
    if len(split) > 0:
        result = shard_levels(rng, extent, split, -0.22, 0.18) * result
    return jnp.clip(result, min=-reach, max=reach).astype(kind)


def setup_inputs(seed: int = 0) -> dict:
    splits = jax.random.split(jax.random.key(seed), 12)
    return {
        "attn_global": bell_draw(splits[0], (MATS, D, D), 1.0, 6.0, ((0, 2), (1, 64), (2, 2)), jnp.float32),
        "attn_momentum": bell_draw(splits[1], (MATS, D, D), 1.0, 6.0, ((0, 2), (1, 64), (2, 2)), jnp.float32),
        "attn_inner": bell_draw(splits[2], (REPS, MATS, D, D), 1.0, 6.0, ((0, 2), (2, 64), (3, 2))),
        "norm_global": jnp.clip(1.0 + 0.1 * jax.random.normal(splits[3], (NORMS, D), jnp.float32), 0.5, 1.5),
        "norm_momentum": bell_draw(splits[4], (NORMS, D), 0.3, 4.0, ((0, 2), (1, 2)), jnp.float32),
        "norm_inner": jnp.clip(1.0 + 0.1 * jax.random.normal(splits[5], (REPS, NORMS, D), jnp.float32), 0.5, 1.5).astype(jnp.bfloat16),
        "emb_global": bell_draw(splits[6], (EMB_BLOCKS, REPS, EMB_ROWS, D), 1.0, 6.0, ((0, 64), (1, 2), (3, 2)), jnp.float32),
        "emb_momentum": bell_draw(splits[7], (EMB_BLOCKS, REPS, EMB_ROWS, D), 1.0, 6.0, ((0, 64), (1, 2), (3, 2)), jnp.float32),
        "emb_inner": bell_draw(splits[8], (REPS, VOCAB, D), 1.0, 6.0, ((0, 2), (1, 64), (2, 2))),
        "basis": bell_draw(splits[9], (D, RANK), D ** -0.5, 0.1875, (), jnp.float32),
        "touched": touch_ends(jax.random.randint(splits[10], (REPS, TOUCHED), 0, VOCAB), jax.random.fold_in(splits[10], 1), 0, VOCAB - 1).astype(jnp.int32),
    }


OUTER_RATE = 0.7
MOMENTUM = 0.9


def nesterov(global_part, momentum_part, outer_grad):
    fresh_momentum = MOMENTUM * momentum_part + outer_grad
    fresh_global = global_part - OUTER_RATE * (outer_grad + MOMENTUM * fresh_momentum)
    return fresh_global, fresh_momentum


def reference(attn_global, attn_momentum, attn_inner, norm_global, norm_momentum, norm_inner, emb_global, emb_momentum, emb_inner, basis, touched):
    groups = REPS * 1.0
    attn_grad = attn_global - jnp.sum(attn_inner.astype(jnp.float32), axis=0) / groups
    new_attn_global, new_attn_momentum = nesterov(attn_global, attn_momentum, attn_grad)
    attn_weights = new_attn_global
    norm_grad = norm_global - jnp.sum(norm_inner.astype(jnp.float32), axis=0) / groups
    new_norm_global, new_norm_momentum = nesterov(norm_global, norm_momentum, norm_grad)
    norm_weights = new_norm_global
    emb_flat = emb_global.reshape(VOCAB, D)
    momentum_flat = emb_momentum.reshape(VOCAB, D)
    group_rows = jnp.broadcast_to(jnp.arange(REPS, dtype=jnp.int32)[:, None], touched.shape)
    touched_masks = jnp.zeros((REPS, VOCAB), jnp.float32).at[group_rows, touched].set(1.0)
    global_coeff = jnp.dot(emb_flat, basis, precision=lax.Precision.HIGHEST, preferred_element_type=jnp.float32)
    coeff_sum = jnp.zeros((VOCAB, RANK), jnp.float32)
    for group in range(REPS):
        inner_coeff = jnp.dot(emb_inner[group].astype(jnp.float32), basis, precision=lax.Precision.HIGHEST, preferred_element_type=jnp.float32)
        coeff_sum = coeff_sum + touched_masks[group][:, None] * (global_coeff - inner_coeff)
    emb_grad = jnp.dot(coeff_sum, basis.T, precision=lax.Precision.HIGHEST, preferred_element_type=jnp.float32) / groups
    flat_global, flat_momentum = nesterov(emb_flat, momentum_flat, emb_grad)
    new_emb_global = flat_global.reshape(EMB_BLOCKS, REPS, EMB_ROWS, D)
    new_emb_momentum = flat_momentum.reshape(EMB_BLOCKS, REPS, EMB_ROWS, D)
    emb_weights = flat_global
    return (new_attn_global, new_attn_momentum, attn_weights, new_norm_global, new_norm_momentum, norm_weights, new_emb_global, new_emb_momentum, emb_weights)
```

```python
import jax
import jax.numpy as jnp
from jax import lax
from jax.sharding import PartitionSpec as P

OUTER_RATE = 0.7
MOMENTUM = 0.9
GROUPS = 2

KEEP = 1.0 - OUTER_RATE * (1.0 + MOMENTUM)
DECAY = OUTER_RATE * MOMENTUM * MOMENTUM
SHARE = OUTER_RATE * (1.0 + MOMENTUM) / GROUPS
STEP = OUTER_RATE * (1.0 + MOMENTUM)

SWAP = [(0, 1), (1, 0)]


def swap(x, axis):
    return lax.ppermute(x, axis, perm=SWAP)


def place_pair(first_is_own, own, other):
    first = jnp.where(first_is_own, own, other)
    second = jnp.where(first_is_own, other, own)
    return jnp.concatenate([first, second], axis=0)


def outer_block(global_part, momentum_part, inner_all, rep_index):
    owned = global_part.shape[0]
    own_inner = lax.dynamic_slice_in_dim(inner_all, rep_index * owned, owned, 0).astype(jnp.float32)
    given_inner = lax.dynamic_slice_in_dim(
        inner_all, (1 - rep_index) * owned, owned, 0
    ).astype(jnp.float32)
    partial = KEEP * global_part - DECAY * momentum_part + SHARE * own_inner
    partial, given_inner, own_inner = lax.optimization_barrier((partial, given_inner, own_inner))
    got_inner = swap(given_inner, "rep")
    got_partial = swap(partial, "rep")
    new_global = partial + SHARE * got_inner
    grad = global_part - (own_inner + got_inner) / GROUPS
    new_momentum = MOMENTUM * momentum_part + grad
    first_is_own = rep_index == 0
    weights = place_pair(first_is_own, partial, got_partial) + SHARE * place_pair(
        first_is_own, got_inner, given_inner
    )
    return new_global, new_momentum, weights


def per_device(
    attn_global,
    attn_momentum,
    attn_inner,
    norm_global,
    norm_momentum,
    norm_inner,
    emb_global,
    emb_momentum,
    emb_inner,
    basis,
    touched,
):
    rep_index = lax.axis_index("rep")
    first_is_own = rep_index == 0
    new_attn_global, new_attn_momentum, attn_weights = outer_block(
        attn_global, attn_momentum, attn_inner[0], rep_index
    )
    new_norm_global, new_norm_momentum, norm_weights = outer_block(
        norm_global, norm_momentum, norm_inner[0], rep_index
    )

    block_rows = emb_inner.shape[1]
    half_rows = emb_global.shape[2]
    half_width = emb_global.shape[3]
    row_start = lax.axis_index("fsdp") * block_rows
    half_start = rep_index * half_rows
    positions = row_start + jnp.arange(block_rows, dtype=jnp.int32)
    matches = touched[:, :, None] == positions[None, None, :]
    touched_masks = jnp.any(matches, axis=1).astype(jnp.float32)
    counts = jnp.sum(touched_masks, axis=0)
    own_mask = lax.dynamic_index_in_dim(touched_masks, rep_index, 0, keepdims=False)
    half_counts = lax.dynamic_slice_in_dim(counts, half_start, half_rows, 0)
    basis_half = lax.dynamic_slice_in_dim(basis, lax.axis_index("tp") * half_width, half_width, 0)
    own_rows = emb_global[0, 0]
    own_momentum = emb_momentum[0, 0]
    kept_rows = own_rows - DECAY * own_momentum
    kept_rows = lax.optimization_barrier(kept_rows)
    got_rows = swap(kept_rows, "rep")
    global_coeff = jnp.dot(
        own_rows, basis_half, precision=lax.Precision.HIGHEST, preferred_element_type=jnp.float32
    )
    inner_coeff = jnp.dot(
        emb_inner[0].astype(jnp.float32),
        basis_half,
        precision=lax.Precision.HIGHEST,
        preferred_element_type=jnp.float32,
    )
    placed_global = place_pair(
        first_is_own, half_counts[:, None] * global_coeff, jnp.zeros_like(global_coeff)
    )
    coeff_term = placed_global - own_mask[:, None] * inner_coeff
    coeff_chip = coeff_term + swap(coeff_term, "tp")
    coeff_sum = coeff_chip + swap(coeff_chip, "rep")
    emb_grad = (
        jnp.dot(
            coeff_sum,
            basis_half.T,
            precision=lax.Precision.HIGHEST,
            preferred_element_type=jnp.float32,
        )
        / GROUPS
    )
    emb_weights = place_pair(first_is_own, kept_rows, got_rows) - STEP * emb_grad
    own_grad = lax.dynamic_slice_in_dim(emb_grad, half_start, half_rows, 0)
    fresh_rows = kept_rows - STEP * own_grad
    fresh_momentum = MOMENTUM * own_momentum + own_grad
    new_emb_global = fresh_rows.reshape(emb_global.shape)
    new_emb_momentum = fresh_momentum.reshape(emb_momentum.shape)
    return (
        new_attn_global,
        new_attn_momentum,
        attn_weights,
        new_norm_global,
        new_norm_momentum,
        norm_weights,
        new_emb_global,
        new_emb_momentum,
        emb_weights,
    )


def solution(mesh):
    placed = (
        P("rep", "fsdp", "tp"),
        P("rep", "fsdp", "tp"),
        P("rep", None, "fsdp", "tp"),
        P("rep", "tp"),
        P("rep", "tp"),
        P("rep", None, "tp"),
        P("fsdp", "rep", None, "tp"),
        P("fsdp", "rep", None, "tp"),
        P("rep", "fsdp", "tp"),
        P(),
        P(),
    )
    return jax.shard_map(
        per_device,
        mesh=mesh,
        in_specs=placed,
        out_specs=(
            P("rep", "fsdp", "tp"),
            P("rep", "fsdp", "tp"),
            P(None, "fsdp", "tp"),
            P("rep", "tp"),
            P("rep", "tp"),
            P(None, "tp"),
            P("fsdp", "rep", None, "tp"),
            P("fsdp", "rep", None, "tp"),
            P("fsdp", "tp"),
        ),
        check_vma=False,
    )
```

```python
import jax
import jax.numpy as jnp
from jax import lax
from jax.sharding import PartitionSpec as P


OUTER_RATE = 0.7
MOMENTUM = 0.9
GROUPS = 2

KEEP = 1.0 - OUTER_RATE * (1.0 + MOMENTUM)
DECAY = OUTER_RATE * MOMENTUM * MOMENTUM
SHARE = OUTER_RATE * (1.0 + MOMENTUM) / GROUPS
STEP = OUTER_RATE * (1.0 + MOMENTUM)

SWAP = [(0, 1), (1, 0)]


def swap(x, axis):
    return lax.ppermute(x, axis, perm=SWAP)


def place_pair(first_is_own, own, other):
    first = jnp.where(first_is_own, own, other)
    second = jnp.where(first_is_own, other, own)
    return jnp.concatenate([first, second], axis=0)


def outer_sends(global_part, momentum_part, inner_all, rep_index):
    owned = global_part.shape[0]
    own_inner = lax.dynamic_slice_in_dim(inner_all, rep_index * owned, owned, 0).astype(jnp.float32)
    given_inner = lax.dynamic_slice_in_dim(
        inner_all, (1 - rep_index) * owned, owned, 0
    ).astype(jnp.float32)
    partial = KEEP * global_part - DECAY * momentum_part + SHARE * own_inner
    return own_inner, given_inner, partial


def outer_finish(global_part, momentum_part, own_inner, given_inner, partial, got_inner, got_partial, first_is_own):
    new_global = partial + SHARE * got_inner
    grad = global_part - (own_inner + got_inner) / GROUPS
    new_momentum = MOMENTUM * momentum_part + grad
    weights = place_pair(first_is_own, partial, got_partial) + SHARE * place_pair(
        first_is_own, got_inner, given_inner
    )
    return new_global, new_momentum, weights


def step_body(
    attn_global,
    attn_momentum,
    attn_inner,
    norm_global,
    norm_momentum,
    norm_inner,
    emb_global,
    emb_momentum,
    emb_inner,
    basis,
    touched,
):
    rep_index = lax.axis_index("rep")
    first_is_own = rep_index == 0
    width = attn_global.shape[-1]
    attn_parts = outer_sends(attn_global, attn_momentum, attn_inner[0], rep_index)
    norm_parts = outer_sends(norm_global, norm_momentum, norm_inner[0], rep_index)
    attn_rows = attn_parts[1].size // width
    norm_rows = norm_parts[1].size // width
    sent = jnp.concatenate(
        [attn_parts[1].reshape(-1, width), attn_parts[2].reshape(-1, width), norm_parts[1], norm_parts[2]],
        axis=0,
    )
    sent = lax.optimization_barrier(sent)
    got = swap(sent, "rep")
    got_attn_inner = got[:attn_rows].reshape(attn_global.shape)
    got_attn_partial = got[attn_rows : 2 * attn_rows].reshape(attn_global.shape)
    got_norm_inner = got[2 * attn_rows : 2 * attn_rows + norm_rows]
    got_norm_partial = got[2 * attn_rows + norm_rows :]
    new_attn_global, new_attn_momentum, attn_weights = outer_finish(
        attn_global, attn_momentum, *attn_parts, got_attn_inner, got_attn_partial, first_is_own
    )
    new_norm_global, new_norm_momentum, norm_weights = outer_finish(
        norm_global, norm_momentum, *norm_parts, got_norm_inner, got_norm_partial, first_is_own
    )

    block_rows = emb_inner.shape[1]
    half_rows = emb_global.shape[2]
    half_width = emb_global.shape[3]
    row_start = lax.axis_index("fsdp") * block_rows
    half_start = rep_index * half_rows
    positions = row_start + jnp.arange(block_rows, dtype=jnp.int32)
    matches = touched[:, :, None] == positions[None, None, :]
    touched_masks = jnp.any(matches, axis=1).astype(jnp.float32)
    counts = jnp.sum(touched_masks, axis=0)
    own_mask = lax.dynamic_index_in_dim(touched_masks, rep_index, 0, keepdims=False)
    half_counts = lax.dynamic_slice_in_dim(counts, half_start, half_rows, 0)
    basis_half = lax.dynamic_slice_in_dim(basis, lax.axis_index("tp") * half_width, half_width, 0)
    own_rows = emb_global[0, 0]
    own_momentum = emb_momentum[0, 0]
    global_coeff = jnp.dot(
        own_rows, basis_half, precision=lax.Precision.HIGHEST, preferred_element_type=jnp.float32
    )
    inner_coeff = jnp.dot(
        emb_inner[0].astype(jnp.float32),
        basis_half,
        precision=lax.Precision.HIGHEST,
        preferred_element_type=jnp.float32,
    )
    placed_global = place_pair(
        first_is_own, half_counts[:, None] * global_coeff, jnp.zeros_like(global_coeff)
    )
    coeff_term = placed_global - own_mask[:, None] * inner_coeff
    coeff_chip = coeff_term + swap(coeff_term, "tp")
    kept_rows = own_rows - DECAY * own_momentum
    kept_rows, coeff_chip = lax.optimization_barrier((kept_rows, coeff_chip))
    coeff_sum = coeff_chip + swap(coeff_chip, "rep")
    got_rows = swap(kept_rows, "rep")
    emb_grad = (
        jnp.dot(
            coeff_sum,
            basis_half.T,
            precision=lax.Precision.HIGHEST,
            preferred_element_type=jnp.float32,
        )
        / GROUPS
    )
    emb_grad = lax.optimization_barrier(emb_grad)
    own_grad = lax.dynamic_slice_in_dim(emb_grad, half_start, half_rows, 0).reshape(emb_global.shape)
    new_emb_global = (emb_global - DECAY * emb_momentum) - STEP * own_grad
    new_emb_momentum = MOMENTUM * emb_momentum + own_grad
    new_emb_global, new_emb_momentum = lax.optimization_barrier((new_emb_global, new_emb_momentum))
    emb_weights = place_pair(first_is_own, kept_rows, got_rows) - STEP * emb_grad
    return (
        new_attn_global,
        new_attn_momentum,
        attn_weights,
        new_norm_global,
        new_norm_momentum,
        norm_weights,
        new_emb_global,
        new_emb_momentum,
        emb_weights,
    )


def solution(mesh):
    placed = (
        P("rep", "fsdp", "tp"),
        P("rep", "fsdp", "tp"),
        P("rep", None, "fsdp", "tp"),
        P("rep", "tp"),
        P("rep", "tp"),
        P("rep", None, "tp"),
        P("fsdp", "rep", None, "tp"),
        P("fsdp", "rep", None, "tp"),
        P("rep", "fsdp", "tp"),
        P(),
        P(),
    )
    return jax.shard_map(
        step_body,
        mesh=mesh,
        in_specs=placed,
        out_specs=(
            P("rep", "fsdp", "tp"),
            P("rep", "fsdp", "tp"),
            P(None, "fsdp", "tp"),
            P("rep", "tp"),
            P("rep", "tp"),
            P(None, "tp"),
            P("fsdp", "rep", None, "tp"),
            P("fsdp", "rep", None, "tp"),
            P("fsdp", "tp"),
        ),
        check_vma=False,
    )
```

```python
import jax
import jax.numpy as jnp
from jax import lax
from jax.sharding import PartitionSpec as P


OUTER_RATE = 0.7
MOMENTUM = 0.9
GROUPS = 2

KEEP = 1.0 - OUTER_RATE * (1.0 + MOMENTUM)
DECAY = OUTER_RATE * MOMENTUM * MOMENTUM
SHARE = OUTER_RATE * (1.0 + MOMENTUM) / GROUPS
STEP = OUTER_RATE * (1.0 + MOMENTUM)

SWAP = [(0, 1), (1, 0)]


def swap(x, axis):
    return lax.ppermute(x, axis, perm=SWAP)


def place_pair(first_is_own, own, other):
    first = jnp.where(first_is_own, own, other)
    second = jnp.where(first_is_own, other, own)
    return jnp.concatenate([first, second], axis=0)


def outer_sends(global_part, inner_all, rep_index):
    owned = global_part.shape[0]
    given_inner = lax.dynamic_slice_in_dim(
        inner_all, (1 - rep_index) * owned, owned, 0
    ).astype(jnp.float32)
    return lax.optimization_barrier(given_inner)


def outer_partial(global_part, momentum_part, inner_all, rep_index):
    owned = global_part.shape[0]
    own_inner = lax.dynamic_slice_in_dim(inner_all, rep_index * owned, owned, 0).astype(jnp.float32)
    partial = KEEP * global_part - DECAY * momentum_part + SHARE * own_inner
    return lax.optimization_barrier((own_inner, partial))


def outer_finish(global_part, momentum_part, own_inner, given_inner, partial, got_inner, got_partial, first_is_own):
    new_global = partial + SHARE * got_inner
    grad = global_part - (own_inner + got_inner) / GROUPS
    new_momentum = MOMENTUM * momentum_part + grad
    weights = place_pair(first_is_own, partial, got_partial) + SHARE * place_pair(
        first_is_own, got_inner, given_inner
    )
    return new_global, new_momentum, weights


def step_body(
    attn_global,
    attn_momentum,
    attn_inner,
    norm_global,
    norm_momentum,
    norm_inner,
    emb_global,
    emb_momentum,
    emb_inner,
    basis,
    touched,
):
    rep_index = lax.axis_index("rep")
    first_is_own = rep_index == 0
    width = attn_global.shape[-1]
    given_attn = outer_sends(attn_global, attn_inner[0], rep_index)
    got_attn_inner = swap(given_attn, "rep")
    given_norm = outer_sends(norm_global, norm_inner[0], rep_index)
    attn_parts = (given_attn,) + outer_partial(attn_global, attn_momentum, attn_inner[0], rep_index)
    norm_parts = (given_norm,) + outer_partial(norm_global, norm_momentum, norm_inner[0], rep_index)
    attn_parts = (attn_parts[1], attn_parts[0], attn_parts[2])
    norm_parts = (norm_parts[1], norm_parts[0], norm_parts[2])
    norm_rows = given_norm.shape[0]
    sent = jnp.concatenate(
        [attn_parts[2].reshape(-1, width), given_norm, norm_parts[2]], axis=0
    )
    sent = lax.optimization_barrier(sent)
    got = swap(sent, "rep")
    attn_rows = attn_parts[2].size // width
    got_attn_partial = got[:attn_rows].reshape(attn_global.shape)
    got_norm_inner = got[attn_rows : attn_rows + norm_rows]
    got_norm_partial = got[attn_rows + norm_rows :]
    new_attn_global, new_attn_momentum, attn_weights = outer_finish(
        attn_global, attn_momentum, *attn_parts, got_attn_inner, got_attn_partial, first_is_own
    )
    new_norm_global, new_norm_momentum, norm_weights = outer_finish(
        norm_global, norm_momentum, *norm_parts, got_norm_inner, got_norm_partial, first_is_own
    )

    block_rows = emb_inner.shape[1]
    half_rows = emb_global.shape[2]
    half_width = emb_global.shape[3]
    row_start = lax.axis_index("fsdp") * block_rows
    half_start = rep_index * half_rows
    positions = row_start + jnp.arange(block_rows, dtype=jnp.int32)
    matches = touched[:, :, None] == positions[None, None, :]
    touched_masks = jnp.any(matches, axis=1).astype(jnp.float32)
    counts = jnp.sum(touched_masks, axis=0)
    own_mask = lax.dynamic_index_in_dim(touched_masks, rep_index, 0, keepdims=False)
    half_counts = lax.dynamic_slice_in_dim(counts, half_start, half_rows, 0)
    basis_half = lax.dynamic_slice_in_dim(basis, lax.axis_index("tp") * half_width, half_width, 0)
    own_rows = emb_global[0, 0]
    own_momentum = emb_momentum[0, 0]
    global_coeff = jnp.dot(
        own_rows, basis_half, precision=lax.Precision.HIGHEST, preferred_element_type=jnp.float32
    )
    inner_coeff = jnp.dot(
        emb_inner[0].astype(jnp.float32),
        basis_half,
        precision=lax.Precision.HIGHEST,
        preferred_element_type=jnp.float32,
    )
    placed_global = place_pair(
        first_is_own, half_counts[:, None] * global_coeff, jnp.zeros_like(global_coeff)
    )
    coeff_term = placed_global - own_mask[:, None] * inner_coeff
    coeff_chip = coeff_term + swap(coeff_term, "tp")
    kept_rows = own_rows - DECAY * own_momentum
    kept_rows, coeff_chip = lax.optimization_barrier((kept_rows, coeff_chip))
    tp_index = lax.axis_index("tp")
    chip_rows = coeff_chip.shape[0] // 2
    coeff_mine = lax.dynamic_slice_in_dim(coeff_chip, tp_index * chip_rows, chip_rows, 0)
    coeff_half = coeff_mine + swap(coeff_mine, "rep")
    coeff_sum = place_pair(tp_index == 0, coeff_half, swap(coeff_half, "tp"))
    got_rows = swap(kept_rows, "rep")
    emb_grad = (
        jnp.dot(
            coeff_sum,
            basis_half.T,
            precision=lax.Precision.HIGHEST,
            preferred_element_type=jnp.float32,
        )
        / GROUPS
    )
    emb_grad = lax.optimization_barrier(emb_grad)
    own_grad = lax.dynamic_slice_in_dim(emb_grad, half_start, half_rows, 0).reshape(emb_global.shape)
    new_emb_global = (emb_global - DECAY * emb_momentum) - STEP * own_grad
    new_emb_momentum = MOMENTUM * emb_momentum + own_grad
    new_emb_global, new_emb_momentum = lax.optimization_barrier((new_emb_global, new_emb_momentum))
    emb_weights = place_pair(first_is_own, kept_rows, got_rows) - STEP * emb_grad
    return (
        new_attn_global,
        new_attn_momentum,
        attn_weights,
        new_norm_global,
        new_norm_momentum,
        norm_weights,
        new_emb_global,
        new_emb_momentum,
        emb_weights,
    )


def solution(mesh):
    placed = (
        P("rep", "fsdp", "tp"),
        P("rep", "fsdp", "tp"),
        P("rep", None, "fsdp", "tp"),
        P("rep", "tp"),
        P("rep", "tp"),
        P("rep", None, "tp"),
        P("fsdp", "rep", None, "tp"),
        P("fsdp", "rep", None, "tp"),
        P("rep", "fsdp", "tp"),
        P(),
        P(),
    )
    return jax.shard_map(
        step_body,
        mesh=mesh,
        in_specs=placed,
        out_specs=(
            P("rep", "fsdp", "tp"),
            P("rep", "fsdp", "tp"),
            P(None, "fsdp", "tp"),
            P("rep", "tp"),
            P("rep", "tp"),
            P(None, "tp"),
            P("fsdp", "rep", None, "tp"),
            P("fsdp", "rep", None, "tp"),
            P("fsdp", "tp"),
        ),
        check_vma=False,
    )
```

```python
import jax
import jax.numpy as jnp
from jax import lax
from jax.sharding import PartitionSpec as P


OUTER_RATE = 0.7
MOMENTUM = 0.9
GROUPS = 2

KEEP = 1.0 - OUTER_RATE * (1.0 + MOMENTUM)
DECAY = OUTER_RATE * MOMENTUM * MOMENTUM
SHARE = OUTER_RATE * (1.0 + MOMENTUM) / GROUPS
STEP = OUTER_RATE * (1.0 + MOMENTUM)

SWAP = [(0, 1), (1, 0)]
LOW = 32


def swap(x, axis):
    return lax.ppermute(x, axis, perm=SWAP)


def place_pair(first_is_own, own, other):
    first = jnp.where(first_is_own, own, other)
    second = jnp.where(first_is_own, other, own)
    return jnp.concatenate([first, second], axis=0)


def outer_sends(global_part, inner_all, rep_index):
    owned = global_part.shape[0]
    given_inner = lax.dynamic_slice_in_dim(
        inner_all, (1 - rep_index) * owned, owned, 0
    ).astype(jnp.float32)
    return lax.optimization_barrier(given_inner)


def outer_partial(global_part, momentum_part, inner_all, rep_index):
    owned = global_part.shape[0]
    own_inner = lax.dynamic_slice_in_dim(inner_all, rep_index * owned, owned, 0).astype(jnp.float32)
    partial = KEEP * global_part - DECAY * momentum_part + SHARE * own_inner
    return lax.optimization_barrier((own_inner, partial))


def outer_finish(global_part, momentum_part, own_inner, given_inner, partial, got_inner, got_partial, first_is_own):
    new_global = partial + SHARE * got_inner
    grad = global_part - (own_inner + got_inner) / GROUPS
    new_momentum = MOMENTUM * momentum_part + grad
    weights = place_pair(first_is_own, partial, got_partial) + SHARE * place_pair(
        first_is_own, got_inner, given_inner
    )
    return new_global, new_momentum, weights


def step_body(
    attn_global,
    attn_momentum,
    attn_inner,
    norm_global,
    norm_momentum,
    norm_inner,
    emb_global,
    emb_momentum,
    emb_inner,
    basis,
    touched,
):
    rep_index = lax.axis_index("rep")
    first_is_own = rep_index == 0
    width = attn_global.shape[-1]
    given_attn = outer_sends(attn_global, attn_inner[0], rep_index)
    got_attn_inner = swap(given_attn, "rep")
    given_norm = outer_sends(norm_global, norm_inner[0], rep_index)
    attn_parts = (given_attn,) + outer_partial(attn_global, attn_momentum, attn_inner[0], rep_index)
    norm_parts = (given_norm,) + outer_partial(norm_global, norm_momentum, norm_inner[0], rep_index)
    attn_parts = (attn_parts[1], attn_parts[0], attn_parts[2])
    norm_parts = (norm_parts[1], norm_parts[0], norm_parts[2])
    sent = lax.optimization_barrier(attn_parts[2])
    norm_sent = jnp.concatenate([given_norm, norm_parts[2]], axis=0)
    got_attn_partial = swap(sent, "rep")
    new_attn_global, new_attn_momentum, attn_weights = outer_finish(
        attn_global, attn_momentum, *attn_parts, got_attn_inner, got_attn_partial, first_is_own
    )

    block_rows = emb_inner.shape[1]
    half_rows = emb_global.shape[2]
    half_width = emb_global.shape[3]
    row_start = lax.axis_index("fsdp") * block_rows
    half_start = rep_index * half_rows
    offsets = touched - row_start
    inside = (offsets >= 0) & (offsets < block_rows)
    high_count = -(-block_rows // LOW)
    high_hot = (
        (offsets[:, None, :] // LOW) == jnp.arange(high_count, dtype=jnp.int32)[None, :, None]
    ) & inside[:, None, :]
    low_hot = (offsets[:, None, :] % LOW) == jnp.arange(LOW, dtype=jnp.int32)[None, :, None]
    hits = jnp.einsum(
        "gik,gjk->gij",
        high_hot.astype(jnp.bfloat16),
        low_hot.astype(jnp.bfloat16),
        preferred_element_type=jnp.float32,
    )
    touched_masks = (hits > 0).astype(jnp.float32).reshape(hits.shape[0], -1)[:, :block_rows]
    counts = jnp.sum(touched_masks, axis=0)
    own_mask = lax.dynamic_index_in_dim(touched_masks, rep_index, 0, keepdims=False)
    half_counts = lax.dynamic_slice_in_dim(counts, half_start, half_rows, 0)
    basis_half = lax.dynamic_slice_in_dim(basis, lax.axis_index("tp") * half_width, half_width, 0)
    own_rows = emb_global[0, 0]
    own_momentum = emb_momentum[0, 0]
    global_coeff = jnp.dot(
        own_rows, basis_half, precision=lax.Precision.HIGHEST, preferred_element_type=jnp.float32
    )
    inner_coeff = jnp.dot(
        emb_inner[0].astype(jnp.float32),
        basis_half,
        precision=lax.Precision.HIGHEST,
        preferred_element_type=jnp.float32,
    )
    placed_global = place_pair(
        first_is_own, half_counts[:, None] * global_coeff, jnp.zeros_like(global_coeff)
    )
    coeff_term = placed_global - own_mask[:, None] * inner_coeff
    coeff_chip = coeff_term + swap(coeff_term, "tp")
    kept_rows = own_rows - DECAY * own_momentum
    kept_rows, coeff_chip = lax.optimization_barrier((kept_rows, coeff_chip))
    tp_index = lax.axis_index("tp")
    chip_rows = coeff_chip.shape[0] // 2
    coeff_mine = lax.dynamic_slice_in_dim(coeff_chip, tp_index * chip_rows, chip_rows, 0)
    coeff_width = coeff_mine.shape[1]
    coeff_sent = jnp.concatenate([coeff_mine, norm_sent.reshape(-1, coeff_width)], axis=0)
    coeff_got = swap(coeff_sent, "rep")
    coeff_half = coeff_mine + coeff_got[:chip_rows]
    norm_rows = given_norm.shape[0]
    norm_got = coeff_got[chip_rows:].reshape(-1, width)
    new_norm_global, new_norm_momentum, norm_weights = outer_finish(
        norm_global, norm_momentum, *norm_parts, norm_got[:norm_rows], norm_got[norm_rows:], first_is_own
    )
    coeff_sum = place_pair(tp_index == 0, coeff_half, swap(coeff_half, "tp"))
    got_rows = swap(kept_rows, "rep")
    emb_grad = (
        jnp.dot(
            coeff_sum,
            basis_half.T,
            precision=lax.Precision.HIGHEST,
            preferred_element_type=jnp.float32,
        )
        / GROUPS
    )
    emb_grad = lax.optimization_barrier(emb_grad)
    own_grad = lax.dynamic_slice_in_dim(emb_grad, half_start, half_rows, 0).reshape(emb_global.shape)
    new_emb_global = (emb_global - DECAY * emb_momentum) - STEP * own_grad
    new_emb_momentum = MOMENTUM * emb_momentum + own_grad
    own_flat = kept_rows - STEP * lax.dynamic_slice_in_dim(emb_grad, half_start, half_rows, 0)
    other_grad = lax.dynamic_slice_in_dim(emb_grad, (1 - rep_index) * half_rows, half_rows, 0)
    new_emb_global, new_emb_momentum, own_flat, other_grad = lax.optimization_barrier(
        (new_emb_global, new_emb_momentum, own_flat, other_grad)
    )
    emb_weights = place_pair(first_is_own, own_flat, got_rows - STEP * other_grad)
    return (
        new_attn_global,
        new_attn_momentum,
        attn_weights,
        new_norm_global,
        new_norm_momentum,
        norm_weights,
        new_emb_global,
        new_emb_momentum,
        emb_weights,
    )


def solution(mesh):
    placed = (
        P("rep", "fsdp", "tp"),
        P("rep", "fsdp", "tp"),
        P("rep", None, "fsdp", "tp"),
        P("rep", "tp"),
        P("rep", "tp"),
        P("rep", None, "tp"),
        P("fsdp", "rep", None, "tp"),
        P("fsdp", "rep", None, "tp"),
        P("rep", "fsdp", "tp"),
        P(),
        P(),
    )
    return jax.shard_map(
        step_body,
        mesh=mesh,
        in_specs=placed,
        out_specs=(
            P("rep", "fsdp", "tp"),
            P("rep", "fsdp", "tp"),
            P(None, "fsdp", "tp"),
            P("rep", "tp"),
            P("rep", "tp"),
            P(None, "tp"),
            P("fsdp", "rep", None, "tp"),
            P("fsdp", "rep", None, "tp"),
            P("fsdp", "tp"),
        ),
        check_vma=False,
    )
```

```python
import jax
import jax.numpy as jnp
from jax import lax
from jax.sharding import PartitionSpec as P


OUTER_RATE = 0.7
MOMENTUM = 0.9
GROUPS = 2

KEEP = 1.0 - OUTER_RATE * (1.0 + MOMENTUM)
DECAY = OUTER_RATE * MOMENTUM * MOMENTUM
SHARE = OUTER_RATE * (1.0 + MOMENTUM) / GROUPS
STEP = OUTER_RATE * (1.0 + MOMENTUM)

SWAP = [(0, 1), (1, 0)]
LOW = 32


def swap(x, axis):
    return lax.ppermute(x, axis, perm=SWAP)


def place_pair(first_is_own, own, other):
    first = jnp.where(first_is_own, own, other)
    second = jnp.where(first_is_own, other, own)
    return jnp.concatenate([first, second], axis=0)


def outer_sends(global_part, inner_all, rep_index):
    owned = global_part.shape[0]
    given_inner = lax.dynamic_slice_in_dim(
        inner_all, (1 - rep_index) * owned, owned, 0
    ).astype(jnp.float32)
    return lax.optimization_barrier(given_inner)


def outer_partial(global_part, momentum_part, inner_all, rep_index):
    owned = global_part.shape[0]
    own_inner = lax.dynamic_slice_in_dim(inner_all, rep_index * owned, owned, 0).astype(jnp.float32)
    partial = KEEP * global_part - DECAY * momentum_part + SHARE * own_inner
    return lax.optimization_barrier((own_inner, partial))


def outer_own(global_part, momentum_part, own_inner, partial, got_inner):
    new_global = partial + SHARE * got_inner
    grad = global_part - (own_inner + got_inner) / GROUPS
    new_momentum = MOMENTUM * momentum_part + grad
    return new_global, new_momentum


def place_own(own, rep_index):
    rows = own.shape[0]
    empty = jnp.zeros((2 * rows,) + own.shape[1:], own.dtype)
    return lax.dynamic_update_slice_in_dim(empty, own, rep_index * rows, 0)


def place_other(placed, other, rep_index):
    rows = other.shape[0]
    return lax.dynamic_update_slice_in_dim(placed, other, (1 - rep_index) * rows, 0)


def step_body(
    attn_global,
    attn_momentum,
    attn_inner,
    norm_global,
    norm_momentum,
    norm_inner,
    emb_global,
    emb_momentum,
    emb_inner,
    basis,
    touched,
):
    rep_index = lax.axis_index("rep")
    first_is_own = rep_index == 0
    width = attn_global.shape[-1]
    given_attn = outer_sends(attn_global, attn_inner[0], rep_index)
    got_attn_inner = swap(given_attn, "rep")
    given_norm = outer_sends(norm_global, norm_inner[0], rep_index)
    attn_parts = (given_attn,) + outer_partial(
        attn_global, attn_momentum, lax.optimization_barrier(attn_inner[0]), rep_index
    )
    norm_parts = (given_norm,) + outer_partial(norm_global, norm_momentum, norm_inner[0], rep_index)
    attn_parts = (attn_parts[1], attn_parts[0], attn_parts[2])
    norm_parts = (norm_parts[1], norm_parts[0], norm_parts[2])
    sent = lax.optimization_barrier(attn_parts[2])
    norm_sent = jnp.concatenate([given_norm, norm_parts[2]], axis=0)
    got_attn_partial = swap(sent, "rep")
    new_attn_global, new_attn_momentum = outer_own(
        attn_global, attn_momentum, attn_parts[0], attn_parts[2], got_attn_inner
    )
    attn_placed = place_own(new_attn_global, rep_index)
    new_attn_global, new_attn_momentum, attn_placed = lax.optimization_barrier(
        (new_attn_global, new_attn_momentum, attn_placed)
    )
    attn_weights = place_other(attn_placed, got_attn_partial + SHARE * given_attn, rep_index)

    block_rows = emb_inner.shape[1]
    half_rows = emb_global.shape[2]
    half_width = emb_global.shape[3]
    row_start = lax.axis_index("fsdp") * block_rows
    half_start = rep_index * half_rows
    offsets = touched - row_start
    inside = (offsets >= 0) & (offsets < block_rows)
    high_count = -(-block_rows // LOW)
    high_hot = (
        (offsets[:, None, :] // LOW) == jnp.arange(high_count, dtype=jnp.int32)[None, :, None]
    ) & inside[:, None, :]
    low_hot = (offsets[:, None, :] % LOW) == jnp.arange(LOW, dtype=jnp.int32)[None, :, None]
    hits = jnp.einsum(
        "gik,gjk->gij",
        high_hot.astype(jnp.bfloat16),
        low_hot.astype(jnp.bfloat16),
        preferred_element_type=jnp.float32,
    )
    touched_masks = (hits > 0).astype(jnp.float32).reshape(hits.shape[0], -1)[:, :block_rows]
    counts = jnp.sum(touched_masks, axis=0)
    own_mask = lax.dynamic_index_in_dim(touched_masks, rep_index, 0, keepdims=False)
    half_counts = lax.dynamic_slice_in_dim(counts, half_start, half_rows, 0)
    basis_half = lax.dynamic_slice_in_dim(basis, lax.axis_index("tp") * half_width, half_width, 0)
    own_rows = emb_global[0, 0]
    own_momentum = emb_momentum[0, 0]
    global_coeff = jnp.dot(
        own_rows, basis_half, precision=lax.Precision.HIGHEST, preferred_element_type=jnp.float32
    )
    inner_coeff = jnp.dot(
        emb_inner[0].astype(jnp.float32),
        basis_half,
        precision=lax.Precision.HIGHEST,
        preferred_element_type=jnp.float32,
    )
    placed_global = place_pair(
        first_is_own, half_counts[:, None] * global_coeff, jnp.zeros_like(global_coeff)
    )
    coeff_term = placed_global - own_mask[:, None] * inner_coeff
    coeff_chip = coeff_term + swap(coeff_term, "tp")
    kept_rows = own_rows - DECAY * own_momentum
    kept_rows, coeff_chip = lax.optimization_barrier((kept_rows, coeff_chip))
    tp_index = lax.axis_index("tp")
    chip_rows = coeff_chip.shape[0] // 2
    coeff_mine = lax.dynamic_slice_in_dim(coeff_chip, tp_index * chip_rows, chip_rows, 0)
    coeff_width = coeff_mine.shape[1]
    coeff_sent = jnp.concatenate([coeff_mine, norm_sent.reshape(-1, coeff_width)], axis=0)
    coeff_got = swap(coeff_sent, "rep")
    coeff_half = coeff_mine + coeff_got[:chip_rows]
    norm_rows = given_norm.shape[0]
    norm_got = coeff_got[chip_rows:].reshape(-1, width)
    new_norm_global, new_norm_momentum = outer_own(
        norm_global, norm_momentum, norm_parts[0], norm_parts[2], norm_got[:norm_rows]
    )
    norm_weights = place_other(
        place_own(new_norm_global, rep_index), norm_got[norm_rows:] + SHARE * given_norm, rep_index
    )
    coeff_sum = place_pair(tp_index == 0, coeff_half, swap(coeff_half, "tp"))
    got_rows = swap(kept_rows, "rep")
    emb_grad = (
        jnp.dot(
            coeff_sum,
            basis_half.T,
            precision=lax.Precision.HIGHEST,
            preferred_element_type=jnp.float32,
        )
        / GROUPS
    )
    emb_grad = lax.optimization_barrier(emb_grad)
    own_grad = lax.dynamic_slice_in_dim(emb_grad, half_start, half_rows, 0).reshape(emb_global.shape)
    new_emb_global = (emb_global - DECAY * emb_momentum) - STEP * own_grad
    new_emb_momentum = MOMENTUM * emb_momentum + own_grad
    own_flat = kept_rows - STEP * lax.dynamic_slice_in_dim(emb_grad, half_start, half_rows, 0)
    other_grad = lax.dynamic_slice_in_dim(emb_grad, (1 - rep_index) * half_rows, half_rows, 0)
    emb_placed = place_own(own_flat, rep_index)
    new_emb_global, new_emb_momentum, emb_placed, other_grad = lax.optimization_barrier(
        (new_emb_global, new_emb_momentum, emb_placed, other_grad)
    )
    emb_weights = place_other(emb_placed, got_rows - STEP * other_grad, rep_index)
    return (
        new_attn_global,
        new_attn_momentum,
        attn_weights,
        new_norm_global,
        new_norm_momentum,
        norm_weights,
        new_emb_global,
        new_emb_momentum,
        emb_weights,
    )


def solution(mesh):
    placed = (
        P("rep", "fsdp", "tp"),
        P("rep", "fsdp", "tp"),
        P("rep", None, "fsdp", "tp"),
        P("rep", "tp"),
        P("rep", "tp"),
        P("rep", None, "tp"),
        P("fsdp", "rep", None, "tp"),
        P("fsdp", "rep", None, "tp"),
        P("rep", "fsdp", "tp"),
        P(),
        P(),
    )
    return jax.shard_map(
        step_body,
        mesh=mesh,
        in_specs=placed,
        out_specs=(
            P("rep", "fsdp", "tp"),
            P("rep", "fsdp", "tp"),
            P(None, "fsdp", "tp"),
            P("rep", "tp"),
            P("rep", "tp"),
            P(None, "tp"),
            P("fsdp", "rep", None, "tp"),
            P("fsdp", "rep", None, "tp"),
            P("fsdp", "tp"),
        ),
        check_vma=False,
    )
```

```python
import jax
import jax.numpy as jnp
from jax import lax
from jax.sharding import PartitionSpec as P


OUTER_RATE = 0.7
MOMENTUM = 0.9
GROUPS = 2

KEEP = 1.0 - OUTER_RATE * (1.0 + MOMENTUM)
DECAY = OUTER_RATE * MOMENTUM * MOMENTUM
SHARE = OUTER_RATE * (1.0 + MOMENTUM) / GROUPS
STEP = OUTER_RATE * (1.0 + MOMENTUM)

SWAP = [(0, 1), (1, 0)]
LOW = 32


def swap(x, axis):
    return lax.ppermute(x, axis, perm=SWAP)


def place_pair(first_is_own, own, other):
    first = jnp.where(first_is_own, own, other)
    second = jnp.where(first_is_own, other, own)
    return jnp.concatenate([first, second], axis=0)


def outer_sends(global_part, inner_all, rep_index):
    owned = global_part.shape[0]
    given_inner = lax.dynamic_slice_in_dim(
        inner_all, (1 - rep_index) * owned, owned, 0
    ).astype(jnp.float32)
    return lax.optimization_barrier(given_inner)


def outer_partial(global_part, momentum_part, inner_all, rep_index):
    owned = global_part.shape[0]
    own_inner = lax.dynamic_slice_in_dim(inner_all, rep_index * owned, owned, 0).astype(jnp.float32)
    partial = KEEP * global_part - DECAY * momentum_part + SHARE * own_inner
    return lax.optimization_barrier((own_inner, partial))


def outer_own(global_part, momentum_part, own_inner, partial, got_inner):
    new_global = partial + SHARE * got_inner
    grad = global_part - (own_inner + got_inner) / GROUPS
    new_momentum = MOMENTUM * momentum_part + grad
    return new_global, new_momentum


def place_own(own, rep_index):
    rows = own.shape[0]
    empty = jnp.zeros((2 * rows,) + own.shape[1:], own.dtype)
    return lax.dynamic_update_slice_in_dim(empty, own, rep_index * rows, 0)


def place_other(placed, other, rep_index):
    rows = other.shape[0]
    return lax.dynamic_update_slice_in_dim(placed, other, (1 - rep_index) * rows, 0)


def step_body(
    attn_global,
    attn_momentum,
    attn_inner,
    norm_global,
    norm_momentum,
    norm_inner,
    emb_global,
    emb_momentum,
    emb_inner,
    basis,
    touched,
):
    rep_index = lax.axis_index("rep")
    first_is_own = rep_index == 0
    width = attn_global.shape[-1]
    given_attn = outer_sends(attn_global, attn_inner[0], rep_index)
    got_attn_inner = swap(given_attn, "rep")
    given_norm = outer_sends(norm_global, norm_inner[0], rep_index)
    attn_parts = (given_attn,) + outer_partial(
        attn_global, attn_momentum, lax.optimization_barrier(attn_inner[0]), rep_index
    )
    norm_parts = (given_norm,) + outer_partial(norm_global, norm_momentum, norm_inner[0], rep_index)
    attn_parts = (attn_parts[1], attn_parts[0], attn_parts[2])
    norm_parts = (norm_parts[1], norm_parts[0], norm_parts[2])
    sent = lax.optimization_barrier(attn_parts[2])
    norm_sent = jnp.concatenate([given_norm, norm_parts[2]], axis=0)
    got_attn_partial = swap(sent, "rep")
    new_attn_global, new_attn_momentum = outer_own(
        attn_global, attn_momentum, attn_parts[0], attn_parts[2], got_attn_inner
    )
    attn_placed = place_own(new_attn_global, rep_index)
    new_attn_global, new_attn_momentum, attn_placed = lax.optimization_barrier(
        (new_attn_global, new_attn_momentum, attn_placed)
    )
    attn_weights = place_other(attn_placed, got_attn_partial + SHARE * given_attn, rep_index)

    block_rows = emb_inner.shape[1]
    half_rows = emb_global.shape[2]
    half_width = emb_global.shape[3]
    row_start = lax.axis_index("fsdp") * block_rows
    half_start = rep_index * half_rows
    offsets = touched - row_start
    inside = (offsets >= 0) & (offsets < block_rows)
    high_count = -(-block_rows // LOW)
    high_hot = (
        (offsets[:, None, :] // LOW) == jnp.arange(high_count, dtype=jnp.int32)[None, :, None]
    ) & inside[:, None, :]
    low_hot = (offsets[:, None, :] % LOW) == jnp.arange(LOW, dtype=jnp.int32)[None, :, None]
    hits = jnp.einsum(
        "gik,gjk->gij",
        high_hot.astype(jnp.bfloat16),
        low_hot.astype(jnp.bfloat16),
        preferred_element_type=jnp.float32,
    )
    touched_masks = (hits > 0).astype(jnp.float32).reshape(hits.shape[0], -1)[:, :block_rows]
    counts = jnp.sum(touched_masks, axis=0)
    own_mask = lax.dynamic_index_in_dim(touched_masks, rep_index, 0, keepdims=False)
    half_counts = lax.dynamic_slice_in_dim(counts, half_start, half_rows, 0)
    basis_half = lax.dynamic_slice_in_dim(basis, lax.axis_index("tp") * half_width, half_width, 0)
    own_rows = emb_global[0, 0]
    own_momentum = emb_momentum[0, 0]
    global_coeff = jnp.dot(
        own_rows, basis_half, precision=lax.Precision.HIGHEST, preferred_element_type=jnp.float32
    )
    inner_coeff = jnp.dot(
        emb_inner[0].astype(jnp.float32),
        basis_half,
        precision=lax.Precision.HIGHEST,
        preferred_element_type=jnp.float32,
    )
    placed_global = place_pair(
        first_is_own, half_counts[:, None] * global_coeff, jnp.zeros_like(global_coeff)
    )
    coeff_term = placed_global - own_mask[:, None] * inner_coeff
    coeff_chip = coeff_term + swap(coeff_term, "tp")
    kept_rows = own_rows - DECAY * own_momentum
    kept_rows, coeff_chip = lax.optimization_barrier((kept_rows, coeff_chip))
    tp_index = lax.axis_index("tp")
    chip_rows = coeff_chip.shape[0] // 2
    coeff_mine = lax.dynamic_slice_in_dim(coeff_chip, tp_index * chip_rows, chip_rows, 0)
    coeff_width = coeff_mine.shape[1]
    coeff_sent = jnp.concatenate([coeff_mine, norm_sent.reshape(-1, coeff_width)], axis=0)
    coeff_got = swap(coeff_sent, "rep")
    coeff_half = coeff_mine + coeff_got[:chip_rows]
    norm_rows = given_norm.shape[0]
    norm_got = coeff_got[chip_rows:].reshape(-1, width)
    new_norm_global, new_norm_momentum = outer_own(
        norm_global, norm_momentum, norm_parts[0], norm_parts[2], norm_got[:norm_rows]
    )
    norm_weights = place_other(
        place_own(new_norm_global, rep_index), norm_got[norm_rows:] + SHARE * given_norm, rep_index
    )
    coeff_sum = place_pair(tp_index == 0, coeff_half, swap(coeff_half, "tp"))
    got_rows = swap(kept_rows, "rep")
    emb_grad = (
        jnp.dot(
            coeff_sum,
            basis_half.T,
            precision=lax.Precision.HIGHEST,
            preferred_element_type=jnp.float32,
        )
        / GROUPS
    )
    emb_grad = lax.optimization_barrier(emb_grad)
    own_grad = lax.dynamic_slice_in_dim(emb_grad, half_start, half_rows, 0).reshape(emb_global.shape)
    new_emb_global = (emb_global - DECAY * emb_momentum) - STEP * own_grad
    new_emb_momentum = MOMENTUM * emb_momentum + own_grad
    own_flat = kept_rows - STEP * lax.dynamic_slice_in_dim(emb_grad, half_start, half_rows, 0)
    other_grad = lax.dynamic_slice_in_dim(emb_grad, (1 - rep_index) * half_rows, half_rows, 0)
    new_emb_global, new_emb_momentum, own_flat, other_grad = lax.optimization_barrier(
        (new_emb_global, new_emb_momentum, own_flat, other_grad)
    )
    emb_weights = place_pair(first_is_own, own_flat, got_rows - STEP * other_grad)
    return (
        new_attn_global,
        new_attn_momentum,
        attn_weights,
        new_norm_global,
        new_norm_momentum,
        norm_weights,
        new_emb_global,
        new_emb_momentum,
        emb_weights,
    )


def solution(mesh):
    placed = (
        P("rep", "fsdp", "tp"),
        P("rep", "fsdp", "tp"),
        P("rep", None, "fsdp", "tp"),
        P("rep", "tp"),
        P("rep", "tp"),
        P("rep", None, "tp"),
        P("fsdp", "rep", None, "tp"),
        P("fsdp", "rep", None, "tp"),
        P("rep", "fsdp", "tp"),
        P(),
        P(),
    )
    return jax.shard_map(
        step_body,
        mesh=mesh,
        in_specs=placed,
        out_specs=(
            P("rep", "fsdp", "tp"),
            P("rep", "fsdp", "tp"),
            P(None, "fsdp", "tp"),
            P("rep", "tp"),
            P("rep", "tp"),
            P(None, "tp"),
            P("fsdp", "rep", None, "tp"),
            P("fsdp", "rep", None, "tp"),
            P("fsdp", "tp"),
        ),
        check_vma=False,
    )
```

```python
import jax
import jax.numpy as jnp
from jax import lax
from jax.sharding import PartitionSpec as P


OUTER_RATE = 0.7
MOMENTUM = 0.9
GROUPS = 2

KEEP = 1.0 - OUTER_RATE * (1.0 + MOMENTUM)
DECAY = OUTER_RATE * MOMENTUM * MOMENTUM
SHARE = OUTER_RATE * (1.0 + MOMENTUM) / GROUPS
STEP = OUTER_RATE * (1.0 + MOMENTUM)

SWAP = [(0, 1), (1, 0)]
LOW = 32


def swap(x, axis):
    return lax.ppermute(x, axis, perm=SWAP)


def place_pair(first_is_own, own, other):
    first = jnp.where(first_is_own, own, other)
    second = jnp.where(first_is_own, other, own)
    return jnp.concatenate([first, second], axis=0)


def outer_sends(global_part, inner_all, rep_index):
    owned = global_part.shape[0]
    given_inner = lax.dynamic_slice_in_dim(
        inner_all, (1 - rep_index) * owned, owned, 0
    ).astype(jnp.float32)
    return lax.optimization_barrier(given_inner)


def outer_partial(global_part, momentum_part, inner_all, rep_index):
    owned = global_part.shape[0]
    own_inner = lax.dynamic_slice_in_dim(inner_all, rep_index * owned, owned, 0).astype(jnp.float32)
    partial = KEEP * global_part - DECAY * momentum_part + SHARE * own_inner
    return lax.optimization_barrier((own_inner, partial))


def outer_own(global_part, momentum_part, own_inner, partial, got_inner):
    new_global = partial + SHARE * got_inner
    grad = global_part - (own_inner + got_inner) / GROUPS
    new_momentum = MOMENTUM * momentum_part + grad
    return new_global, new_momentum


def place_own(own, rep_index):
    rows = own.shape[0]
    empty = jnp.zeros((2 * rows,) + own.shape[1:], own.dtype)
    return lax.dynamic_update_slice_in_dim(empty, own, rep_index * rows, 0)


def place_other(placed, other, rep_index):
    rows = other.shape[0]
    return lax.dynamic_update_slice_in_dim(placed, other, (1 - rep_index) * rows, 0)


def step_body(
    attn_global,
    attn_momentum,
    attn_inner,
    norm_global,
    norm_momentum,
    norm_inner,
    emb_global,
    emb_momentum,
    emb_inner,
    basis,
    touched,
):
    rep_index = lax.axis_index("rep")
    first_is_own = rep_index == 0
    width = attn_global.shape[-1]
    given_attn = outer_sends(attn_global, attn_inner[0], rep_index)
    got_attn_inner = swap(given_attn, "rep")
    given_norm = outer_sends(norm_global, norm_inner[0], rep_index)
    attn_parts = (given_attn,) + outer_partial(
        attn_global, attn_momentum, lax.optimization_barrier(attn_inner[0]), rep_index
    )
    norm_parts = (given_norm,) + outer_partial(norm_global, norm_momentum, norm_inner[0], rep_index)
    attn_parts = (attn_parts[1], attn_parts[0], attn_parts[2])
    norm_parts = (norm_parts[1], norm_parts[0], norm_parts[2])
    attn_rows = attn_parts[2].size // width
    norm_rows = given_norm.shape[0]
    sent = jnp.concatenate([attn_parts[2].reshape(-1, width), given_norm, norm_parts[2]], axis=0)
    sent = lax.optimization_barrier(sent)
    got_buffer = swap(sent, "rep")
    new_attn_global, new_attn_momentum = outer_own(
        attn_global, attn_momentum, attn_parts[0], attn_parts[2], got_attn_inner
    )
    attn_placed = place_own(new_attn_global, rep_index)
    new_attn_global, new_attn_momentum, attn_placed = lax.optimization_barrier(
        (new_attn_global, new_attn_momentum, attn_placed)
    )
    attn_other = got_buffer[:attn_rows] + SHARE * given_attn.reshape(-1, width)
    attn_weights = place_other(attn_placed, attn_other.reshape(attn_global.shape), rep_index)
    norm_got = got_buffer[attn_rows:]
    new_norm_global, new_norm_momentum = outer_own(
        norm_global, norm_momentum, norm_parts[0], norm_parts[2], norm_got[:norm_rows]
    )
    norm_weights = place_other(
        place_own(new_norm_global, rep_index), norm_got[norm_rows:] + SHARE * given_norm, rep_index
    )

    block_rows = emb_inner.shape[1]
    half_rows = emb_global.shape[2]
    half_width = emb_global.shape[3]
    row_start = lax.axis_index("fsdp") * block_rows
    half_start = rep_index * half_rows
    offsets = touched - row_start
    inside = (offsets >= 0) & (offsets < block_rows)
    high_count = -(-block_rows // LOW)
    high_hot = (
        (offsets[:, None, :] // LOW) == jnp.arange(high_count, dtype=jnp.int32)[None, :, None]
    ) & inside[:, None, :]
    low_hot = (offsets[:, None, :] % LOW) == jnp.arange(LOW, dtype=jnp.int32)[None, :, None]
    hits = jnp.einsum(
        "gik,gjk->gij",
        high_hot.astype(jnp.bfloat16),
        low_hot.astype(jnp.bfloat16),
        preferred_element_type=jnp.float32,
    )
    touched_masks = (hits > 0).astype(jnp.float32).reshape(hits.shape[0], -1)[:, :block_rows]
    counts = jnp.sum(touched_masks, axis=0)
    own_mask = lax.dynamic_index_in_dim(touched_masks, rep_index, 0, keepdims=False)
    half_counts = lax.dynamic_slice_in_dim(counts, half_start, half_rows, 0)
    basis_half = lax.dynamic_slice_in_dim(basis, lax.axis_index("tp") * half_width, half_width, 0)
    own_rows = emb_global[0, 0]
    own_momentum = emb_momentum[0, 0]
    global_coeff = jnp.dot(
        own_rows, basis_half, precision=lax.Precision.HIGHEST, preferred_element_type=jnp.float32
    )
    inner_coeff = jnp.dot(
        emb_inner[0].astype(jnp.float32),
        basis_half,
        precision=lax.Precision.HIGHEST,
        preferred_element_type=jnp.float32,
    )
    placed_global = place_pair(
        first_is_own, half_counts[:, None] * global_coeff, jnp.zeros_like(global_coeff)
    )
    coeff_term = placed_global - own_mask[:, None] * inner_coeff
    tp_index = lax.axis_index("tp")
    chip_rows = coeff_term.shape[0] // 2
    coeff_given = lax.dynamic_slice_in_dim(coeff_term, (1 - tp_index) * chip_rows, chip_rows, 0)
    coeff_kept = lax.dynamic_slice_in_dim(coeff_term, tp_index * chip_rows, chip_rows, 0)
    coeff_mine = coeff_kept + swap(coeff_given, "tp")
    kept_rows = own_rows - DECAY * own_momentum
    kept_rows, coeff_mine = lax.optimization_barrier((kept_rows, coeff_mine))
    coeff_half = coeff_mine + swap(coeff_mine, "rep")
    coeff_sum = place_pair(tp_index == 0, coeff_half, swap(coeff_half, "tp"))
    got_rows = swap(kept_rows, "rep")
    emb_grad = (
        jnp.dot(
            coeff_sum,
            basis_half.T,
            precision=lax.Precision.HIGHEST,
            preferred_element_type=jnp.float32,
        )
        / GROUPS
    )
    emb_grad = lax.optimization_barrier(emb_grad)
    own_grad = lax.dynamic_slice_in_dim(emb_grad, half_start, half_rows, 0).reshape(emb_global.shape)
    new_emb_global = (emb_global - DECAY * emb_momentum) - STEP * own_grad
    new_emb_momentum = MOMENTUM * emb_momentum + own_grad
    own_flat = kept_rows - STEP * lax.dynamic_slice_in_dim(emb_grad, half_start, half_rows, 0)
    other_grad = lax.dynamic_slice_in_dim(emb_grad, (1 - rep_index) * half_rows, half_rows, 0)
    new_emb_global, new_emb_momentum, own_flat, other_grad = lax.optimization_barrier(
        (new_emb_global, new_emb_momentum, own_flat, other_grad)
    )
    emb_weights = place_pair(first_is_own, own_flat, got_rows - STEP * other_grad)
    return (
        new_attn_global,
        new_attn_momentum,
        attn_weights,
        new_norm_global,
        new_norm_momentum,
        norm_weights,
        new_emb_global,
        new_emb_momentum,
        emb_weights,
    )


def solution(mesh):
    placed = (
        P("rep", "fsdp", "tp"),
        P("rep", "fsdp", "tp"),
        P("rep", None, "fsdp", "tp"),
        P("rep", "tp"),
        P("rep", "tp"),
        P("rep", None, "tp"),
        P("fsdp", "rep", None, "tp"),
        P("fsdp", "rep", None, "tp"),
        P("rep", "fsdp", "tp"),
        P(),
        P(),
    )
    return jax.shard_map(
        step_body,
        mesh=mesh,
        in_specs=placed,
        out_specs=(
            P("rep", "fsdp", "tp"),
            P("rep", "fsdp", "tp"),
            P(None, "fsdp", "tp"),
            P("rep", "tp"),
            P("rep", "tp"),
            P(None, "tp"),
            P("fsdp", "rep", None, "tp"),
            P("fsdp", "rep", None, "tp"),
            P("fsdp", "tp"),
        ),
        check_vma=False,
    )
```

```python
import jax
import jax.numpy as jnp
from jax import lax
from jax.sharding import PartitionSpec as P


OUTER_RATE = 0.7
MOMENTUM = 0.9
GROUPS = 2

KEEP = 1.0 - OUTER_RATE * (1.0 + MOMENTUM)
DECAY = OUTER_RATE * MOMENTUM * MOMENTUM
SHARE = OUTER_RATE * (1.0 + MOMENTUM) / GROUPS
STEP = OUTER_RATE * (1.0 + MOMENTUM)

SWAP = [(0, 1), (1, 0)]
LOW = 32


def swap(x, axis):
    return lax.ppermute(x, axis, perm=SWAP)


def place_pair(first_is_own, own, other):
    first = jnp.where(first_is_own, own, other)
    second = jnp.where(first_is_own, other, own)
    return jnp.concatenate([first, second], axis=0)


def outer_sends(global_part, inner_all, rep_index):
    owned = global_part.shape[0]
    given_inner = lax.dynamic_slice_in_dim(
        inner_all, (1 - rep_index) * owned, owned, 0
    ).astype(jnp.float32)
    return lax.optimization_barrier(given_inner)


def outer_partial(global_part, momentum_part, inner_all, rep_index):
    owned = global_part.shape[0]
    own_inner = lax.dynamic_slice_in_dim(inner_all, rep_index * owned, owned, 0).astype(jnp.float32)
    partial = KEEP * global_part - DECAY * momentum_part + SHARE * own_inner
    return lax.optimization_barrier((own_inner, partial))


def outer_own(global_part, momentum_part, own_inner, partial, got_inner):
    new_global = partial + SHARE * got_inner
    grad = global_part - (own_inner + got_inner) / GROUPS
    new_momentum = MOMENTUM * momentum_part + grad
    return new_global, new_momentum


def place_own(own, rep_index):
    rows = own.shape[0]
    empty = jnp.zeros((2 * rows,) + own.shape[1:], own.dtype)
    return lax.dynamic_update_slice_in_dim(empty, own, rep_index * rows, 0)


def place_other(placed, other, rep_index):
    rows = other.shape[0]
    return lax.dynamic_update_slice_in_dim(placed, other, (1 - rep_index) * rows, 0)


def step_body(
    attn_global,
    attn_momentum,
    attn_inner,
    norm_global,
    norm_momentum,
    norm_inner,
    emb_global,
    emb_momentum,
    emb_inner,
    basis,
    touched,
):
    rep_index = lax.axis_index("rep")
    first_is_own = rep_index == 0
    width = attn_global.shape[-1]
    given_attn = outer_sends(attn_global, attn_inner[0], rep_index)
    got_attn_inner = swap(given_attn, "rep")
    given_norm = outer_sends(norm_global, norm_inner[0], rep_index)
    attn_parts = (given_attn,) + outer_partial(
        attn_global, attn_momentum, lax.optimization_barrier(attn_inner[0]), rep_index
    )
    norm_parts = (given_norm,) + outer_partial(norm_global, norm_momentum, norm_inner[0], rep_index)
    attn_parts = (attn_parts[1], attn_parts[0], attn_parts[2])
    norm_parts = (norm_parts[1], norm_parts[0], norm_parts[2])
    attn_rows = attn_parts[2].size // width
    norm_rows = given_norm.shape[0]
    sent = jnp.concatenate([attn_parts[2].reshape(-1, width), given_norm, norm_parts[2]], axis=0)
    sent = lax.optimization_barrier(sent)
    got_buffer = swap(sent, "rep")
    new_attn_global, new_attn_momentum = outer_own(
        attn_global, attn_momentum, attn_parts[0], attn_parts[2], got_attn_inner
    )
    attn_placed = place_own(new_attn_global, rep_index)
    new_attn_global, new_attn_momentum, attn_placed = lax.optimization_barrier(
        (new_attn_global, new_attn_momentum, attn_placed)
    )
    attn_other = got_buffer[:attn_rows] + SHARE * given_attn.reshape(-1, width)
    attn_weights = place_other(attn_placed, attn_other.reshape(attn_global.shape), rep_index)
    norm_got = got_buffer[attn_rows:]
    new_norm_global, new_norm_momentum = outer_own(
        norm_global, norm_momentum, norm_parts[0], norm_parts[2], norm_got[:norm_rows]
    )
    norm_weights = place_other(
        place_own(new_norm_global, rep_index), norm_got[norm_rows:] + SHARE * given_norm, rep_index
    )

    block_rows = emb_inner.shape[1]
    half_rows = emb_global.shape[2]
    half_width = emb_global.shape[3]
    row_start = lax.axis_index("fsdp") * block_rows
    half_start = rep_index * half_rows
    offsets = touched - row_start
    inside = (offsets >= 0) & (offsets < block_rows)
    high_count = -(-block_rows // LOW)
    high_hot = (
        (offsets[:, None, :] // LOW) == jnp.arange(high_count, dtype=jnp.int32)[None, :, None]
    ) & inside[:, None, :]
    low_hot = (offsets[:, None, :] % LOW) == jnp.arange(LOW, dtype=jnp.int32)[None, :, None]
    hits = jnp.einsum(
        "gik,gjk->gij",
        high_hot.astype(jnp.bfloat16),
        low_hot.astype(jnp.bfloat16),
        preferred_element_type=jnp.float32,
    )
    touched_masks = (hits > 0).astype(jnp.float32).reshape(hits.shape[0], -1)[:, :block_rows]
    counts = jnp.sum(touched_masks, axis=0)
    own_mask = lax.dynamic_index_in_dim(touched_masks, rep_index, 0, keepdims=False)
    half_counts = lax.dynamic_slice_in_dim(counts, half_start, half_rows, 0)
    basis_half = lax.dynamic_slice_in_dim(basis, lax.axis_index("tp") * half_width, half_width, 0)
    own_rows = emb_global[0, 0]
    own_momentum = emb_momentum[0, 0]
    global_coeff = jnp.dot(
        own_rows, basis_half, precision=lax.Precision.HIGHEST, preferred_element_type=jnp.float32
    )
    inner_coeff = jnp.dot(
        emb_inner[0].astype(jnp.float32),
        basis_half,
        precision=lax.Precision.HIGHEST,
        preferred_element_type=jnp.float32,
    )
    placed_global = place_pair(
        first_is_own, half_counts[:, None] * global_coeff, jnp.zeros_like(global_coeff)
    )
    coeff_term = placed_global - own_mask[:, None] * inner_coeff
    tp_index = lax.axis_index("tp")
    chip_rows = coeff_term.shape[0] // 2
    coeff_given = lax.dynamic_slice_in_dim(coeff_term, (1 - tp_index) * chip_rows, chip_rows, 0)
    coeff_kept = lax.dynamic_slice_in_dim(coeff_term, tp_index * chip_rows, chip_rows, 0)
    coeff_mine = coeff_kept + swap(coeff_given, "tp")
    kept_rows = own_rows - DECAY * own_momentum
    kept_rows, coeff_mine = lax.optimization_barrier((kept_rows, coeff_mine))
    coeff_half = coeff_mine + swap(coeff_mine, "rep")
    coeff_sum = place_pair(tp_index == 0, coeff_half, swap(coeff_half, "tp"))
    got_rows = swap(kept_rows, "rep")
    emb_grad = (
        jnp.dot(
            coeff_sum,
            basis_half.T,
            precision=lax.Precision.HIGHEST,
            preferred_element_type=jnp.float32,
        )
        / GROUPS
    )
    emb_grad = lax.optimization_barrier(emb_grad)
    own_grad = lax.dynamic_slice_in_dim(emb_grad, half_start, half_rows, 0).reshape(emb_global.shape)
    new_emb_global = (emb_global - DECAY * emb_momentum) - STEP * own_grad
    new_emb_momentum = MOMENTUM * emb_momentum + own_grad
    own_flat = kept_rows - STEP * lax.dynamic_slice_in_dim(emb_grad, half_start, half_rows, 0)
    other_grad = lax.dynamic_slice_in_dim(emb_grad, (1 - rep_index) * half_rows, half_rows, 0)
    new_emb_global, new_emb_momentum, own_flat, other_grad = lax.optimization_barrier(
        (new_emb_global, new_emb_momentum, own_flat, other_grad)
    )
    row_ids = lax.broadcasted_iota(jnp.int32, (block_rows, half_width), 0)
    in_own_half = (row_ids >= half_start) & (row_ids < half_start + half_rows)
    emb_weights = jnp.where(
        in_own_half,
        jnp.concatenate([own_flat, own_flat], axis=0),
        jnp.concatenate([got_rows, got_rows], axis=0)
        - STEP * jnp.concatenate([other_grad, other_grad], axis=0),
    )
    return (
        new_attn_global,
        new_attn_momentum,
        attn_weights,
        new_norm_global,
        new_norm_momentum,
        norm_weights,
        new_emb_global,
        new_emb_momentum,
        emb_weights,
    )


def solution(mesh):
    placed = (
        P("rep", "fsdp", "tp"),
        P("rep", "fsdp", "tp"),
        P("rep", None, "fsdp", "tp"),
        P("rep", "tp"),
        P("rep", "tp"),
        P("rep", None, "tp"),
        P("fsdp", "rep", None, "tp"),
        P("fsdp", "rep", None, "tp"),
        P("rep", "fsdp", "tp"),
        P(),
        P(),
    )
    return jax.shard_map(
        step_body,
        mesh=mesh,
        in_specs=placed,
        out_specs=(
            P("rep", "fsdp", "tp"),
            P("rep", "fsdp", "tp"),
            P(None, "fsdp", "tp"),
            P("rep", "tp"),
            P("rep", "tp"),
            P(None, "tp"),
            P("fsdp", "rep", None, "tp"),
            P("fsdp", "rep", None, "tp"),
            P("fsdp", "tp"),
        ),
        check_vma=False,
    )
```

```python
import jax
import jax.numpy as jnp
from jax import lax
from jax.sharding import PartitionSpec as P


OUTER_RATE = 0.7
MOMENTUM = 0.9
GROUPS = 2

KEEP = 1.0 - OUTER_RATE * (1.0 + MOMENTUM)
DECAY = OUTER_RATE * MOMENTUM * MOMENTUM
SHARE = OUTER_RATE * (1.0 + MOMENTUM) / GROUPS
STEP = OUTER_RATE * (1.0 + MOMENTUM)

SWAP = [(0, 1), (1, 0)]
LOW = 32


def swap(x, axis):
    return lax.ppermute(x, axis, perm=SWAP)


def place_pair(first_is_own, own, other):
    first = jnp.where(first_is_own, own, other)
    second = jnp.where(first_is_own, other, own)
    return jnp.concatenate([first, second], axis=0)


def outer_sends(global_part, inner_all, rep_index):
    owned = global_part.shape[0]
    given_inner = lax.dynamic_slice_in_dim(
        inner_all, (1 - rep_index) * owned, owned, 0
    ).astype(jnp.float32)
    return lax.optimization_barrier(given_inner)


def outer_partial(global_part, momentum_part, inner_all, rep_index):
    owned = global_part.shape[0]
    own_inner = lax.dynamic_slice_in_dim(inner_all, rep_index * owned, owned, 0).astype(jnp.float32)
    partial = KEEP * global_part - DECAY * momentum_part + SHARE * own_inner
    return lax.optimization_barrier((own_inner, partial))


def outer_own(global_part, momentum_part, own_inner, partial, got_inner):
    new_global = partial + SHARE * got_inner
    grad = global_part - (own_inner + got_inner) / GROUPS
    new_momentum = MOMENTUM * momentum_part + grad
    return new_global, new_momentum


def place_own(own, rep_index):
    rows = own.shape[0]
    empty = jnp.zeros((2 * rows,) + own.shape[1:], own.dtype)
    return lax.dynamic_update_slice_in_dim(empty, own, rep_index * rows, 0)


def place_other(placed, other, rep_index):
    rows = other.shape[0]
    return lax.dynamic_update_slice_in_dim(placed, other, (1 - rep_index) * rows, 0)


def step_body(
    attn_global,
    attn_momentum,
    attn_inner,
    norm_global,
    norm_momentum,
    norm_inner,
    emb_global,
    emb_momentum,
    emb_inner,
    basis,
    touched,
):
    rep_index = lax.axis_index("rep")
    first_is_own = rep_index == 0
    own_rows = emb_global[0, 0]
    own_momentum = emb_momentum[0, 0]
    kept_rows = own_rows - DECAY * own_momentum
    given_norm = outer_sends(norm_global, norm_inner[0], rep_index)
    norm_parts = (given_norm,) + outer_partial(norm_global, norm_momentum, norm_inner[0], rep_index)
    norm_parts = (norm_parts[1], norm_parts[0], norm_parts[2])
    half_rows = kept_rows.shape[0]
    norm_rows = given_norm.shape[0]
    rows_sent = jnp.concatenate([kept_rows, given_norm, norm_parts[2]], axis=0)
    kept_rows, rows_sent = lax.optimization_barrier((kept_rows, rows_sent))
    rows_got = swap(rows_sent, "rep")
    got_rows = rows_got[:half_rows]
    norm_got = rows_got[half_rows:]
    given_attn = outer_sends(attn_global, attn_inner[0], rep_index)
    got_attn_inner = swap(given_attn, "rep")
    attn_parts = (given_attn,) + outer_partial(
        attn_global, attn_momentum, lax.optimization_barrier(attn_inner[0]), rep_index
    )
    attn_parts = (attn_parts[1], attn_parts[0], attn_parts[2])
    got_attn_partial = swap(attn_parts[2], "rep")
    new_attn_global, new_attn_momentum = outer_own(
        attn_global, attn_momentum, attn_parts[0], attn_parts[2], got_attn_inner
    )
    attn_placed = place_own(new_attn_global, rep_index)
    new_attn_global, new_attn_momentum, attn_placed = lax.optimization_barrier(
        (new_attn_global, new_attn_momentum, attn_placed)
    )
    attn_weights = place_other(attn_placed, got_attn_partial + SHARE * given_attn, rep_index)
    new_norm_global, new_norm_momentum = outer_own(
        norm_global, norm_momentum, norm_parts[0], norm_parts[2], norm_got[:norm_rows]
    )
    norm_weights = place_other(
        place_own(new_norm_global, rep_index), norm_got[norm_rows:] + SHARE * given_norm, rep_index
    )

    block_rows = emb_inner.shape[1]
    half_width = emb_global.shape[3]
    row_start = lax.axis_index("fsdp") * block_rows
    half_start = rep_index * half_rows
    offsets = touched - row_start
    inside = (offsets >= 0) & (offsets < block_rows)
    high_count = -(-block_rows // LOW)
    high_hot = (
        (offsets[:, None, :] // LOW) == jnp.arange(high_count, dtype=jnp.int32)[None, :, None]
    ) & inside[:, None, :]
    low_hot = (offsets[:, None, :] % LOW) == jnp.arange(LOW, dtype=jnp.int32)[None, :, None]
    hits = jnp.einsum(
        "gik,gjk->gij",
        high_hot.astype(jnp.bfloat16),
        low_hot.astype(jnp.bfloat16),
        preferred_element_type=jnp.float32,
    )
    touched_masks = (hits > 0).astype(jnp.float32).reshape(hits.shape[0], -1)[:, :block_rows]
    counts = jnp.sum(touched_masks, axis=0)
    own_mask = lax.dynamic_index_in_dim(touched_masks, rep_index, 0, keepdims=False)
    half_counts = lax.dynamic_slice_in_dim(counts, half_start, half_rows, 0)
    basis_half = lax.dynamic_slice_in_dim(basis, lax.axis_index("tp") * half_width, half_width, 0)
    global_coeff = jnp.dot(
        own_rows, basis_half, precision=lax.Precision.HIGHEST, preferred_element_type=jnp.float32
    )
    inner_coeff = jnp.dot(
        emb_inner[0].astype(jnp.float32),
        basis_half,
        precision=lax.Precision.HIGHEST,
        preferred_element_type=jnp.float32,
    )
    placed_global = place_pair(
        first_is_own, half_counts[:, None] * global_coeff, jnp.zeros_like(global_coeff)
    )
    coeff_term = placed_global - own_mask[:, None] * inner_coeff
    tp_index = lax.axis_index("tp")
    chip_rows = coeff_term.shape[0] // 2
    coeff_given = lax.dynamic_slice_in_dim(coeff_term, (1 - tp_index) * chip_rows, chip_rows, 0)
    coeff_kept = lax.dynamic_slice_in_dim(coeff_term, tp_index * chip_rows, chip_rows, 0)
    coeff_mine = coeff_kept + swap(coeff_given, "tp")
    coeff_half = coeff_mine + swap(coeff_mine, "rep")
    coeff_sum = place_pair(tp_index == 0, coeff_half, swap(coeff_half, "tp"))
    emb_grad = (
        jnp.dot(
            coeff_sum,
            basis_half.T,
            precision=lax.Precision.HIGHEST,
            preferred_element_type=jnp.float32,
        )
        / GROUPS
    )
    emb_grad = lax.optimization_barrier(emb_grad)
    own_grad = lax.dynamic_slice_in_dim(emb_grad, half_start, half_rows, 0).reshape(emb_global.shape)
    new_emb_global = (emb_global - DECAY * emb_momentum) - STEP * own_grad
    new_emb_momentum = MOMENTUM * emb_momentum + own_grad
    own_flat = kept_rows - STEP * lax.dynamic_slice_in_dim(emb_grad, half_start, half_rows, 0)
    other_grad = lax.dynamic_slice_in_dim(emb_grad, (1 - rep_index) * half_rows, half_rows, 0)
    new_emb_global, new_emb_momentum, own_flat, other_grad = lax.optimization_barrier(
        (new_emb_global, new_emb_momentum, own_flat, other_grad)
    )
    emb_weights = place_pair(first_is_own, own_flat, got_rows - STEP * other_grad)
    return (
        new_attn_global,
        new_attn_momentum,
        attn_weights,
        new_norm_global,
        new_norm_momentum,
        norm_weights,
        new_emb_global,
        new_emb_momentum,
        emb_weights,
    )


def solution(mesh):
    placed = (
        P("rep", "fsdp", "tp"),
        P("rep", "fsdp", "tp"),
        P("rep", None, "fsdp", "tp"),
        P("rep", "tp"),
        P("rep", "tp"),
        P("rep", None, "tp"),
        P("fsdp", "rep", None, "tp"),
        P("fsdp", "rep", None, "tp"),
        P("rep", "fsdp", "tp"),
        P(),
        P(),
    )
    return jax.shard_map(
        step_body,
        mesh=mesh,
        in_specs=placed,
        out_specs=(
            P("rep", "fsdp", "tp"),
            P("rep", "fsdp", "tp"),
            P(None, "fsdp", "tp"),
            P("rep", "tp"),
            P("rep", "tp"),
            P(None, "tp"),
            P("fsdp", "rep", None, "tp"),
            P("fsdp", "rep", None, "tp"),
            P("fsdp", "tp"),
        ),
        check_vma=False,
    )
```

```python
import jax
import jax.numpy as jnp
from jax import lax
from jax.sharding import PartitionSpec as P


OUTER_RATE = 0.7
MOMENTUM = 0.9
GROUPS = 2

KEEP = 1.0 - OUTER_RATE * (1.0 + MOMENTUM)
DECAY = OUTER_RATE * MOMENTUM * MOMENTUM
SHARE = OUTER_RATE * (1.0 + MOMENTUM) / GROUPS
STEP = OUTER_RATE * (1.0 + MOMENTUM)

SWAP = [(0, 1), (1, 0)]
LOW = 32


def swap(x, axis):
    return lax.ppermute(x, axis, perm=SWAP)


def place_pair(first_is_own, own, other):
    first = jnp.where(first_is_own, own, other)
    second = jnp.where(first_is_own, other, own)
    return jnp.concatenate([first, second], axis=0)


def outer_sends(global_part, inner_all, rep_index):
    owned = global_part.shape[0]
    given_inner = lax.dynamic_slice_in_dim(
        inner_all, (1 - rep_index) * owned, owned, 0
    ).astype(jnp.float32)
    return lax.optimization_barrier(given_inner)


def outer_partial(global_part, momentum_part, inner_all, rep_index):
    owned = global_part.shape[0]
    own_inner = lax.dynamic_slice_in_dim(inner_all, rep_index * owned, owned, 0).astype(jnp.float32)
    partial = KEEP * global_part - DECAY * momentum_part + SHARE * own_inner
    return lax.optimization_barrier((own_inner, partial))


def outer_own(global_part, momentum_part, own_inner, partial, got_inner):
    new_global = partial + SHARE * got_inner
    grad = global_part - (own_inner + got_inner) / GROUPS
    new_momentum = MOMENTUM * momentum_part + grad
    return new_global, new_momentum


def place_own(own, rep_index):
    rows = own.shape[0]
    empty = jnp.zeros((2 * rows,) + own.shape[1:], own.dtype)
    return lax.dynamic_update_slice_in_dim(empty, own, rep_index * rows, 0)


def place_other(placed, other, rep_index):
    rows = other.shape[0]
    return lax.dynamic_update_slice_in_dim(placed, other, (1 - rep_index) * rows, 0)


def step_body(
    attn_global,
    attn_momentum,
    attn_inner,
    norm_global,
    norm_momentum,
    norm_inner,
    emb_global,
    emb_momentum,
    emb_inner,
    basis,
    touched,
):
    rep_index = lax.axis_index("rep")
    first_is_own = rep_index == 0
    width = attn_global.shape[-1]
    given_attn = outer_sends(attn_global, attn_inner[0], rep_index)
    got_attn_inner = swap(given_attn, "rep")
    given_norm = outer_sends(norm_global, norm_inner[0], rep_index)
    attn_parts = (given_attn,) + outer_partial(
        attn_global, attn_momentum, lax.optimization_barrier(attn_inner[0]), rep_index
    )
    norm_parts = (given_norm,) + outer_partial(norm_global, norm_momentum, norm_inner[0], rep_index)
    attn_parts = (attn_parts[1], attn_parts[0], attn_parts[2])
    norm_parts = (norm_parts[1], norm_parts[0], norm_parts[2])
    attn_rows = attn_parts[2].size // width
    norm_rows = given_norm.shape[0]
    sent = jnp.concatenate([attn_parts[2].reshape(-1, width), given_norm, norm_parts[2]], axis=0)
    sent = lax.optimization_barrier(sent)
    got_buffer = swap(sent, "rep")
    new_attn_global, new_attn_momentum = outer_own(
        attn_global, attn_momentum, attn_parts[0], attn_parts[2], got_attn_inner
    )
    attn_placed = place_own(new_attn_global, rep_index)
    new_attn_global, new_attn_momentum, attn_placed = lax.optimization_barrier(
        (new_attn_global, new_attn_momentum, attn_placed)
    )
    attn_other = got_buffer[:attn_rows] + SHARE * given_attn.reshape(-1, width)
    attn_weights = place_other(attn_placed, attn_other.reshape(attn_global.shape), rep_index)
    norm_got = got_buffer[attn_rows:]
    new_norm_global, new_norm_momentum = outer_own(
        norm_global, norm_momentum, norm_parts[0], norm_parts[2], norm_got[:norm_rows]
    )
    norm_weights = place_other(
        place_own(new_norm_global, rep_index), norm_got[norm_rows:] + SHARE * given_norm, rep_index
    )

    block_rows = emb_inner.shape[1]
    half_rows = emb_global.shape[2]
    half_width = emb_global.shape[3]
    row_start = lax.axis_index("fsdp") * block_rows
    half_start = rep_index * half_rows
    offsets = touched - row_start
    inside = (offsets >= 0) & (offsets < block_rows)
    high_count = -(-block_rows // LOW)
    high_hot = (
        (offsets[:, None, :] // LOW) == jnp.arange(high_count, dtype=jnp.int32)[None, :, None]
    ) & inside[:, None, :]
    low_hot = (offsets[:, None, :] % LOW) == jnp.arange(LOW, dtype=jnp.int32)[None, :, None]
    hits = jnp.einsum(
        "gik,gjk->gij",
        high_hot.astype(jnp.bfloat16),
        low_hot.astype(jnp.bfloat16),
        preferred_element_type=jnp.float32,
    )
    touched_masks = (hits > 0).astype(jnp.float32).reshape(hits.shape[0], -1)[:, :block_rows]
    counts = jnp.sum(touched_masks, axis=0)
    own_mask = lax.dynamic_index_in_dim(touched_masks, rep_index, 0, keepdims=False)
    half_counts = lax.dynamic_slice_in_dim(counts, half_start, half_rows, 0)
    basis_half = lax.dynamic_slice_in_dim(basis, lax.axis_index("tp") * half_width, half_width, 0)
    own_rows = emb_global[0, 0]
    own_momentum = emb_momentum[0, 0]
    global_coeff = jnp.dot(
        own_rows, basis_half, precision=lax.Precision.HIGHEST, preferred_element_type=jnp.float32
    )
    inner_coeff = jnp.dot(
        emb_inner[0].astype(jnp.float32),
        basis_half,
        precision=lax.Precision.HIGHEST,
        preferred_element_type=jnp.float32,
    )
    placed_global = place_pair(
        first_is_own, half_counts[:, None] * global_coeff, jnp.zeros_like(global_coeff)
    )
    coeff_term = placed_global - own_mask[:, None] * inner_coeff
    tp_index = lax.axis_index("tp")
    chip_rows = coeff_term.shape[0] // 2
    coeff_given = lax.dynamic_slice_in_dim(coeff_term, (1 - tp_index) * chip_rows, chip_rows, 0)
    coeff_kept = lax.dynamic_slice_in_dim(coeff_term, tp_index * chip_rows, chip_rows, 0)
    coeff_mine = coeff_kept + swap(coeff_given, "tp")
    kept_rows = own_rows - DECAY * own_momentum
    kept_rows, coeff_mine = lax.optimization_barrier((kept_rows, coeff_mine))
    coeff_half = coeff_mine + swap(coeff_mine, "rep")
    coeff_sum = place_pair(tp_index == 0, coeff_half, swap(coeff_half, "tp"))
    lead = half_rows % 8
    pad_rows = lead + half_rows + (-(lead + half_rows)) % 8
    shifted = jnp.pad(kept_rows, ((lead, pad_rows - lead - half_rows), (0, 0)))
    plain = jnp.pad(kept_rows, ((0, pad_rows - half_rows), (0, 0)))
    rows_sent = jnp.where(rep_index == 1, shifted, plain)
    got_rows = swap(rows_sent, "rep")
    emb_grad = (
        jnp.dot(
            coeff_sum,
            basis_half.T,
            precision=lax.Precision.HIGHEST,
            preferred_element_type=jnp.float32,
        )
        / GROUPS
    )
    emb_grad = lax.optimization_barrier(emb_grad)
    own_grad = lax.dynamic_slice_in_dim(emb_grad, half_start, half_rows, 0).reshape(emb_global.shape)
    new_emb_global = (emb_global - DECAY * emb_momentum) - STEP * own_grad
    new_emb_momentum = MOMENTUM * emb_momentum + own_grad
    own_flat = kept_rows - STEP * lax.dynamic_slice_in_dim(emb_grad, half_start, half_rows, 0)
    other_grad = lax.dynamic_slice_in_dim(emb_grad, (1 - rep_index) * half_rows, half_rows, 0)
    own_full = place_pair(first_is_own, own_flat, jnp.zeros_like(own_flat))
    new_emb_global, new_emb_momentum, own_full = lax.optimization_barrier(
        (new_emb_global, new_emb_momentum, own_full)
    )
    aligned_start = half_rows - lead
    other_full = jnp.where(
        first_is_own,
        jnp.concatenate(
            [jnp.zeros((aligned_start, half_width), jnp.float32), got_rows[: block_rows - aligned_start]],
            axis=0,
        ),
        jnp.concatenate(
            [got_rows, jnp.zeros((block_rows - pad_rows, half_width), jnp.float32)], axis=0
        ),
    )
    row_ids = lax.broadcasted_iota(jnp.int32, (block_rows, half_width), 0)
    in_own_half = (row_ids >= half_start) & (row_ids < half_start + half_rows)
    emb_weights = jnp.where(in_own_half, own_full, other_full - STEP * emb_grad)
    return (
        new_attn_global,
        new_attn_momentum,
        attn_weights,
        new_norm_global,
        new_norm_momentum,
        norm_weights,
        new_emb_global,
        new_emb_momentum,
        emb_weights,
    )


def solution(mesh):
    placed = (
        P("rep", "fsdp", "tp"),
        P("rep", "fsdp", "tp"),
        P("rep", None, "fsdp", "tp"),
        P("rep", "tp"),
        P("rep", "tp"),
        P("rep", None, "tp"),
        P("fsdp", "rep", None, "tp"),
        P("fsdp", "rep", None, "tp"),
        P("rep", "fsdp", "tp"),
        P(),
        P(),
    )
    return jax.shard_map(
        step_body,
        mesh=mesh,
        in_specs=placed,
        out_specs=(
            P("rep", "fsdp", "tp"),
            P("rep", "fsdp", "tp"),
            P(None, "fsdp", "tp"),
            P("rep", "tp"),
            P("rep", "tp"),
            P(None, "tp"),
            P("fsdp", "rep", None, "tp"),
            P("fsdp", "rep", None, "tp"),
            P("fsdp", "tp"),
        ),
        check_vma=False,
    )
```

```python
import jax
import jax.numpy as jnp
from jax import lax
from jax.sharding import PartitionSpec as P


OUTER_RATE = 0.7
MOMENTUM = 0.9
GROUPS = 2

KEEP = 1.0 - OUTER_RATE * (1.0 + MOMENTUM)
DECAY = OUTER_RATE * MOMENTUM * MOMENTUM
SHARE = OUTER_RATE * (1.0 + MOMENTUM) / GROUPS
STEP = OUTER_RATE * (1.0 + MOMENTUM)

SWAP = [(0, 1), (1, 0)]
LOW = 32


def swap(x, axis):
    return lax.ppermute(x, axis, perm=SWAP)


def place_pair(first_is_own, own, other):
    first = jnp.where(first_is_own, own, other)
    second = jnp.where(first_is_own, other, own)
    return jnp.concatenate([first, second], axis=0)


def outer_sends(global_part, inner_all, rep_index):
    owned = global_part.shape[0]
    given_inner = lax.dynamic_slice_in_dim(
        inner_all, (1 - rep_index) * owned, owned, 0
    ).astype(jnp.float32)
    return lax.optimization_barrier(given_inner)


def outer_partial(global_part, momentum_part, inner_all, rep_index):
    owned = global_part.shape[0]
    own_inner = lax.dynamic_slice_in_dim(inner_all, rep_index * owned, owned, 0).astype(jnp.float32)
    partial = KEEP * global_part - DECAY * momentum_part + SHARE * own_inner
    return lax.optimization_barrier((own_inner, partial))


def outer_own(global_part, momentum_part, own_inner, partial, got_inner):
    new_global = partial + SHARE * got_inner
    grad = global_part - (own_inner + got_inner) / GROUPS
    new_momentum = MOMENTUM * momentum_part + grad
    return new_global, new_momentum


def place_own(own, rep_index):
    rows = own.shape[0]
    empty = jnp.zeros((2 * rows,) + own.shape[1:], own.dtype)
    return lax.dynamic_update_slice_in_dim(empty, own, rep_index * rows, 0)


def place_other(placed, other, rep_index):
    rows = other.shape[0]
    return lax.dynamic_update_slice_in_dim(placed, other, (1 - rep_index) * rows, 0)


def step_body(
    attn_global,
    attn_momentum,
    attn_inner,
    norm_global,
    norm_momentum,
    norm_inner,
    emb_global,
    emb_momentum,
    emb_inner,
    basis,
    touched,
):
    rep_index = lax.axis_index("rep")
    first_is_own = rep_index == 0
    width = attn_global.shape[-1]
    owned = attn_global.shape[0]
    first_mats = owned // 3
    given_start = (1 - rep_index) * owned
    given_head = lax.optimization_barrier(
        lax.dynamic_slice_in_dim(attn_inner[0], given_start, first_mats, 0).astype(jnp.float32)
    )
    got_head = swap(given_head, "rep")
    given_tail = lax.optimization_barrier(
        lax.dynamic_slice_in_dim(
            attn_inner[0], given_start + first_mats, owned - first_mats, 0
        ).astype(jnp.float32)
    )
    got_tail = swap(given_tail, "rep")
    given_attn = jnp.concatenate([given_head, given_tail], axis=0)
    got_attn_inner = jnp.concatenate([got_head, got_tail], axis=0)
    given_norm = outer_sends(norm_global, norm_inner[0], rep_index)
    attn_parts = (given_attn,) + outer_partial(
        attn_global, attn_momentum, lax.optimization_barrier(attn_inner[0]), rep_index
    )
    norm_parts = (given_norm,) + outer_partial(norm_global, norm_momentum, norm_inner[0], rep_index)
    attn_parts = (attn_parts[1], attn_parts[0], attn_parts[2])
    norm_parts = (norm_parts[1], norm_parts[0], norm_parts[2])
    attn_rows = attn_parts[2].size // width
    norm_rows = given_norm.shape[0]
    sent = jnp.concatenate([attn_parts[2].reshape(-1, width), given_norm, norm_parts[2]], axis=0)
    sent = lax.optimization_barrier(sent)
    got_buffer = swap(sent, "rep")
    new_attn_global, new_attn_momentum = outer_own(
        attn_global, attn_momentum, attn_parts[0], attn_parts[2], got_attn_inner
    )
    attn_placed = place_own(new_attn_global, rep_index)
    new_attn_global, new_attn_momentum, attn_placed = lax.optimization_barrier(
        (new_attn_global, new_attn_momentum, attn_placed)
    )
    attn_other = got_buffer[:attn_rows] + SHARE * given_attn.reshape(-1, width)
    attn_weights = place_other(attn_placed, attn_other.reshape(attn_global.shape), rep_index)
    norm_got = got_buffer[attn_rows:]
    new_norm_global, new_norm_momentum = outer_own(
        norm_global, norm_momentum, norm_parts[0], norm_parts[2], norm_got[:norm_rows]
    )
    norm_weights = place_other(
        place_own(new_norm_global, rep_index), norm_got[norm_rows:] + SHARE * given_norm, rep_index
    )

    block_rows = emb_inner.shape[1]
    half_rows = emb_global.shape[2]
    half_width = emb_global.shape[3]
    row_start = lax.axis_index("fsdp") * block_rows
    half_start = rep_index * half_rows
    offsets = touched - row_start
    inside = (offsets >= 0) & (offsets < block_rows)
    high_count = -(-block_rows // LOW)
    high_hot = (
        (offsets[:, None, :] // LOW) == jnp.arange(high_count, dtype=jnp.int32)[None, :, None]
    ) & inside[:, None, :]
    low_hot = (offsets[:, None, :] % LOW) == jnp.arange(LOW, dtype=jnp.int32)[None, :, None]
    hits = jnp.einsum(
        "gik,gjk->gij",
        high_hot.astype(jnp.bfloat16),
        low_hot.astype(jnp.bfloat16),
        preferred_element_type=jnp.float32,
    )
    touched_masks = (hits > 0).astype(jnp.float32).reshape(hits.shape[0], -1)[:, :block_rows]
    counts = jnp.sum(touched_masks, axis=0)
    own_mask = lax.dynamic_index_in_dim(touched_masks, rep_index, 0, keepdims=False)
    half_counts = lax.dynamic_slice_in_dim(counts, half_start, half_rows, 0)
    basis_half = lax.dynamic_slice_in_dim(basis, lax.axis_index("tp") * half_width, half_width, 0)
    own_rows = emb_global[0, 0]
    own_momentum = emb_momentum[0, 0]
    global_coeff = jnp.dot(
        own_rows, basis_half, precision=lax.Precision.HIGHEST, preferred_element_type=jnp.float32
    )
    inner_coeff = jnp.dot(
        emb_inner[0].astype(jnp.float32),
        basis_half,
        precision=lax.Precision.HIGHEST,
        preferred_element_type=jnp.float32,
    )
    placed_global = place_pair(
        first_is_own, half_counts[:, None] * global_coeff, jnp.zeros_like(global_coeff)
    )
    coeff_term = placed_global - own_mask[:, None] * inner_coeff
    tp_index = lax.axis_index("tp")
    chip_rows = coeff_term.shape[0] // 2
    coeff_given = lax.dynamic_slice_in_dim(coeff_term, (1 - tp_index) * chip_rows, chip_rows, 0)
    coeff_kept = lax.dynamic_slice_in_dim(coeff_term, tp_index * chip_rows, chip_rows, 0)
    coeff_mine = coeff_kept + swap(coeff_given, "tp")
    kept_rows = own_rows - DECAY * own_momentum
    kept_rows, coeff_mine = lax.optimization_barrier((kept_rows, coeff_mine))
    coeff_half = coeff_mine + swap(coeff_mine, "rep")
    coeff_sum = place_pair(tp_index == 0, coeff_half, swap(coeff_half, "tp"))
    lead = half_rows % 8
    pad_rows = lead + half_rows + (-(lead + half_rows)) % 8
    shifted = jnp.pad(kept_rows, ((lead, pad_rows - lead - half_rows), (0, 0)))
    plain = jnp.pad(kept_rows, ((0, pad_rows - half_rows), (0, 0)))
    rows_sent = jnp.where(rep_index == 1, shifted, plain)
    got_rows = swap(rows_sent, "rep")
    emb_grad = (
        jnp.dot(
            coeff_sum,
            basis_half.T,
            precision=lax.Precision.HIGHEST,
            preferred_element_type=jnp.float32,
        )
        / GROUPS
    )
    emb_grad = lax.optimization_barrier(emb_grad)
    own_grad = lax.dynamic_slice_in_dim(emb_grad, half_start, half_rows, 0).reshape(emb_global.shape)
    new_emb_global = (emb_global - DECAY * emb_momentum) - STEP * own_grad
    new_emb_momentum = MOMENTUM * emb_momentum + own_grad
    own_flat = kept_rows - STEP * lax.dynamic_slice_in_dim(emb_grad, half_start, half_rows, 0)
    other_grad = lax.dynamic_slice_in_dim(emb_grad, (1 - rep_index) * half_rows, half_rows, 0)
    own_full = place_pair(first_is_own, own_flat, jnp.zeros_like(own_flat))
    new_emb_global, new_emb_momentum, own_full = lax.optimization_barrier(
        (new_emb_global, new_emb_momentum, own_full)
    )
    aligned_start = half_rows - lead
    other_full = jnp.where(
        first_is_own,
        jnp.concatenate(
            [jnp.zeros((aligned_start, half_width), jnp.float32), got_rows[: block_rows - aligned_start]],
            axis=0,
        ),
        jnp.concatenate(
            [got_rows, jnp.zeros((block_rows - pad_rows, half_width), jnp.float32)], axis=0
        ),
    )
    row_ids = lax.broadcasted_iota(jnp.int32, (block_rows, half_width), 0)
    in_own_half = (row_ids >= half_start) & (row_ids < half_start + half_rows)
    emb_weights = jnp.where(in_own_half, own_full, other_full - STEP * emb_grad)
    return (
        new_attn_global,
        new_attn_momentum,
        attn_weights,
        new_norm_global,
        new_norm_momentum,
        norm_weights,
        new_emb_global,
        new_emb_momentum,
        emb_weights,
    )


def solution(mesh):
    placed = (
        P("rep", "fsdp", "tp"),
        P("rep", "fsdp", "tp"),
        P("rep", None, "fsdp", "tp"),
        P("rep", "tp"),
        P("rep", "tp"),
        P("rep", None, "tp"),
        P("fsdp", "rep", None, "tp"),
        P("fsdp", "rep", None, "tp"),
        P("rep", "fsdp", "tp"),
        P(),
        P(),
    )
    return jax.shard_map(
        step_body,
        mesh=mesh,
        in_specs=placed,
        out_specs=(
            P("rep", "fsdp", "tp"),
            P("rep", "fsdp", "tp"),
            P(None, "fsdp", "tp"),
            P("rep", "tp"),
            P("rep", "tp"),
            P(None, "tp"),
            P("fsdp", "rep", None, "tp"),
            P("fsdp", "rep", None, "tp"),
            P("fsdp", "tp"),
        ),
        check_vma=False,
    )
```

```python
import jax
import jax.numpy as jnp
from jax import lax
from jax.sharding import PartitionSpec as P


OUTER_RATE = 0.7
MOMENTUM = 0.9
GROUPS = 2

KEEP = 1.0 - OUTER_RATE * (1.0 + MOMENTUM)
DECAY = OUTER_RATE * MOMENTUM * MOMENTUM
SHARE = OUTER_RATE * (1.0 + MOMENTUM) / GROUPS
STEP = OUTER_RATE * (1.0 + MOMENTUM)

SWAP = [(0, 1), (1, 0)]
LOW = 32


def swap(x, axis):
    return lax.ppermute(x, axis, perm=SWAP)


def place_pair(first_is_own, own, other):
    first = jnp.where(first_is_own, own, other)
    second = jnp.where(first_is_own, other, own)
    return jnp.concatenate([first, second], axis=0)


def outer_sends(global_part, inner_all, rep_index):
    owned = global_part.shape[0]
    given_inner = lax.dynamic_slice_in_dim(
        inner_all, (1 - rep_index) * owned, owned, 0
    ).astype(jnp.float32)
    return lax.optimization_barrier(given_inner)


def outer_partial(global_part, momentum_part, inner_all, rep_index):
    owned = global_part.shape[0]
    own_inner = lax.dynamic_slice_in_dim(inner_all, rep_index * owned, owned, 0).astype(jnp.float32)
    partial = KEEP * global_part - DECAY * momentum_part + SHARE * own_inner
    return lax.optimization_barrier((own_inner, partial))


def outer_own(global_part, momentum_part, own_inner, partial, got_inner):
    new_global = partial + SHARE * got_inner
    grad = global_part - (own_inner + got_inner) / GROUPS
    new_momentum = MOMENTUM * momentum_part + grad
    return new_global, new_momentum


def place_own(own, rep_index):
    rows = own.shape[0]
    empty = jnp.zeros((2 * rows,) + own.shape[1:], own.dtype)
    return lax.dynamic_update_slice_in_dim(empty, own, rep_index * rows, 0)


def place_other(placed, other, rep_index):
    rows = other.shape[0]
    return lax.dynamic_update_slice_in_dim(placed, other, (1 - rep_index) * rows, 0)


def step_body(
    attn_global,
    attn_momentum,
    attn_inner,
    norm_global,
    norm_momentum,
    norm_inner,
    emb_global,
    emb_momentum,
    emb_inner,
    basis,
    touched,
):
    rep_index = lax.axis_index("rep")
    first_is_own = rep_index == 0
    width = attn_global.shape[-1]
    given_attn = outer_sends(attn_global, attn_inner[0], rep_index)
    got_attn_inner = swap(given_attn, "rep")
    given_norm = outer_sends(norm_global, norm_inner[0], rep_index)
    attn_parts = (given_attn,) + outer_partial(
        attn_global, attn_momentum, lax.optimization_barrier(attn_inner[0]), rep_index
    )
    norm_parts = (given_norm,) + outer_partial(norm_global, norm_momentum, norm_inner[0], rep_index)
    attn_parts = (attn_parts[1], attn_parts[0], attn_parts[2])
    norm_parts = (norm_parts[1], norm_parts[0], norm_parts[2])
    attn_rows = attn_parts[2].size // width
    norm_rows = given_norm.shape[0]
    sent = jnp.concatenate([attn_parts[2].reshape(-1, width), given_norm, norm_parts[2]], axis=0)
    sent = lax.optimization_barrier(sent)
    got_buffer = swap(sent, "rep")
    new_attn_global, new_attn_momentum = outer_own(
        attn_global, attn_momentum, attn_parts[0], attn_parts[2], got_attn_inner
    )
    attn_placed = place_own(new_attn_global, rep_index)
    new_attn_global, new_attn_momentum, attn_placed = lax.optimization_barrier(
        (new_attn_global, new_attn_momentum, attn_placed)
    )
    attn_other = got_buffer[:attn_rows] + SHARE * given_attn.reshape(-1, width)
    attn_weights = place_other(attn_placed, attn_other.reshape(attn_global.shape), rep_index)
    norm_got = got_buffer[attn_rows:]
    new_norm_global, new_norm_momentum = outer_own(
        norm_global, norm_momentum, norm_parts[0], norm_parts[2], norm_got[:norm_rows]
    )
    norm_weights = place_other(
        place_own(new_norm_global, rep_index), norm_got[norm_rows:] + SHARE * given_norm, rep_index
    )

    block_rows = emb_inner.shape[1]
    half_rows = emb_global.shape[2]
    half_width = emb_global.shape[3]
    row_start = lax.axis_index("fsdp") * block_rows
    half_start = rep_index * half_rows
    offsets = touched - row_start
    inside = (offsets >= 0) & (offsets < block_rows)
    high_count = -(-block_rows // LOW)
    high_hot = (
        (offsets[:, None, :] // LOW) == jnp.arange(high_count, dtype=jnp.int32)[None, :, None]
    ) & inside[:, None, :]
    low_hot = (offsets[:, None, :] % LOW) == jnp.arange(LOW, dtype=jnp.int32)[None, :, None]
    hits = jnp.einsum(
        "gik,gjk->gij",
        high_hot.astype(jnp.bfloat16),
        low_hot.astype(jnp.bfloat16),
        preferred_element_type=jnp.float32,
    )
    touched_masks = (hits > 0).astype(jnp.float32).reshape(hits.shape[0], -1)[:, :block_rows]
    counts = jnp.sum(touched_masks, axis=0)
    own_mask = lax.dynamic_index_in_dim(touched_masks, rep_index, 0, keepdims=False)
    half_counts = lax.dynamic_slice_in_dim(counts, half_start, half_rows, 0)
    basis_half = lax.dynamic_slice_in_dim(basis, lax.axis_index("tp") * half_width, half_width, 0)
    own_rows = emb_global[0, 0]
    own_momentum = emb_momentum[0, 0]
    global_coeff = jnp.dot(
        own_rows, basis_half, precision=lax.Precision.HIGHEST, preferred_element_type=jnp.float32
    )
    inner_coeff = jnp.dot(
        emb_inner[0].astype(jnp.float32),
        basis_half,
        precision=lax.Precision.HIGHEST,
        preferred_element_type=jnp.float32,
    )
    placed_global = place_pair(
        first_is_own, half_counts[:, None] * global_coeff, jnp.zeros_like(global_coeff)
    )
    coeff_term = placed_global - own_mask[:, None] * inner_coeff
    tp_index = lax.axis_index("tp")
    chip_rows = coeff_term.shape[0] // 2
    coeff_given = lax.dynamic_slice_in_dim(coeff_term, (1 - tp_index) * chip_rows, chip_rows, 0)
    coeff_kept = lax.dynamic_slice_in_dim(coeff_term, tp_index * chip_rows, chip_rows, 0)
    coeff_mine = coeff_kept + swap(coeff_given, "tp")
    kept_rows = own_rows - DECAY * own_momentum
    kept_rows, coeff_mine = lax.optimization_barrier((kept_rows, coeff_mine))
    coeff_half = coeff_mine + swap(coeff_mine, "rep")
    coeff_sum = place_pair(tp_index == 0, coeff_half, swap(coeff_half, "tp"))
    lead = half_rows % 8
    pad_rows = lead + half_rows + (-(lead + half_rows)) % 8
    shifted = jnp.pad(kept_rows, ((lead, pad_rows - lead - half_rows), (0, 0)))
    plain = jnp.pad(kept_rows, ((0, pad_rows - half_rows), (0, 0)))
    rows_sent = jnp.where(rep_index == 1, shifted, plain)
    got_rows = swap(rows_sent, "rep")
    emb_grad = (
        jnp.dot(
            coeff_sum,
            basis_half.T,
            precision=lax.Precision.HIGHEST,
            preferred_element_type=jnp.float32,
        )
        / GROUPS
    )
    emb_grad = lax.optimization_barrier(emb_grad)
    own_grad = lax.dynamic_slice_in_dim(emb_grad, half_start, half_rows, 0).reshape(emb_global.shape)
    new_emb_global = (emb_global - DECAY * emb_momentum) - STEP * own_grad
    new_emb_momentum = MOMENTUM * emb_momentum + own_grad
    own_flat = kept_rows - STEP * lax.dynamic_slice_in_dim(emb_grad, half_start, half_rows, 0)
    other_grad = lax.dynamic_slice_in_dim(emb_grad, (1 - rep_index) * half_rows, half_rows, 0)
    own_full = place_pair(first_is_own, own_flat, jnp.zeros_like(own_flat))
    aligned_start = half_rows - lead
    span = block_rows - aligned_start
    update_start = (1 - rep_index) * aligned_start
    own_part = lax.dynamic_slice_in_dim(own_full, update_start, span, 0)
    grad_part = lax.dynamic_slice_in_dim(emb_grad, update_start, span, 0)
    new_emb_global, new_emb_momentum, own_full, own_part, grad_part = lax.optimization_barrier(
        (new_emb_global, new_emb_momentum, own_full, own_part, grad_part)
    )
    part_rows = update_start + lax.broadcasted_iota(jnp.int32, (span, half_width), 0)
    in_own_half = (part_rows >= half_start) & (part_rows < half_start + half_rows)
    update = jnp.where(in_own_half, own_part, got_rows[:span] - STEP * grad_part)
    emb_weights = lax.dynamic_update_slice_in_dim(own_full, update, update_start, 0)
    return (
        new_attn_global,
        new_attn_momentum,
        attn_weights,
        new_norm_global,
        new_norm_momentum,
        norm_weights,
        new_emb_global,
        new_emb_momentum,
        emb_weights,
    )


def solution(mesh):
    placed = (
        P("rep", "fsdp", "tp"),
        P("rep", "fsdp", "tp"),
        P("rep", None, "fsdp", "tp"),
        P("rep", "tp"),
        P("rep", "tp"),
        P("rep", None, "tp"),
        P("fsdp", "rep", None, "tp"),
        P("fsdp", "rep", None, "tp"),
        P("rep", "fsdp", "tp"),
        P(),
        P(),
    )
    return jax.shard_map(
        step_body,
        mesh=mesh,
        in_specs=placed,
        out_specs=(
            P("rep", "fsdp", "tp"),
            P("rep", "fsdp", "tp"),
            P(None, "fsdp", "tp"),
            P("rep", "tp"),
            P("rep", "tp"),
            P(None, "tp"),
            P("fsdp", "rep", None, "tp"),
            P("fsdp", "rep", None, "tp"),
            P("fsdp", "tp"),
        ),
        check_vma=False,
    )
```
